256 devices in a mesh: section: 4 (over x_hi, core), expert: 4 (over y), dp: 16 (over z, x_lo).
Axes of the slice: x: 4 (x_hi: 2, x_lo: 2; x = x_hi * 2 + x_lo), y: 4, z: 8, core: 2. Of those that a mesh axis runs over, the one named last changes fastest.
Arguments:
- tokens: bfloat16 [2, 4096, 3072], P(None, ('expert', 'dp')), may hold values from -6 to 6
- routes: int32 [2, 4096, 2], P(None, ('expert', 'dp')), may hold values from 0 to 3, all different within a row; in each aligned block of 64 rows (0 to 63, 64 to 127, ..., all dimensions but the last counted through in order) at most 36 rows name the same one
- router: bfloat16 [3072, 4], replicated, may hold values from -0.109375 to 0.109375
- gate_weight: bfloat16 [4, 8192, 3072], P('expert', ('section', 'dp')), may hold values from -0.109375 to 0.109375
- up_weight: bfloat16 [4, 8192, 3072], P('expert', ('section', 'dp')), may hold values from -0.109375 to 0.109375
- down_weight: bfloat16 [4, 8192, 3072], P('expert', ('section', 'dp')), may hold values from -0.0625 to 0.0625
Outputs:
- activations: bfloat16 [2, 4096, 3072], P(None, ('expert', 'dp'), 'section')
- gram: bfloat16 [4, 3072, 3072], P('expert', ('section', 'dp'))
The draws below stay inside these ranges and needn't reach their ends.
Inputs may be any that keep to these rules, and one draw needn't show every extreme that they name: `routes`: in every micro-batch, each aligned block of 64 tokens (the tokens of one device) names no expert more than 36 times, a bound that some block reaches; the two experts of a token differ; every expert is named somewhere.
All inputs are finite; a program needn't handle non-finite values.
Results may differ from the reference program's by a relative error of at most 0.02.
Values may be sent and summed in bfloat16 or wider, within the bound.
No kernel may reach another device: no remote copies, remote signals or barrier semaphores. Data moves between devices by JAX's collectives and lax.ppermute only.
A program may use at most 128 MiB of HBM per device.

```python
import math
import jax
import jax.numpy as jnp
import numpy as np
from jax import lax

D = 3072
FW = 8192
MB = 2
TOK_DEV = 64
EXPERTS = 4
CAP = 36
TOKENS = 4096
N_EXPERT = 4
N_DP = 16


def levels(key, extent, split, least, high):
    loudness, own = 1.0, jax.random.fold_in(key, 6)
    for position, blocks in split:
        draws = jnp.exp(jax.random.uniform(jax.random.fold_in(own, position), (blocks,), jnp.float32, least / len(split), high / len(split)))
        loudness = loudness * jnp.repeat(draws, extent[position] // blocks).reshape([-1 if axis == position else 1 for axis in range(len(extent))])
    return loudness


def shared_out(stream_key, own, number, rows, count, top, reach, lean):
    order = jax.random.permutation(stream_key, count)
    crowded, ordinary = shares(count, rows * top, reach, lean, True), shares(count, rows * top, reach, lean, False)
    places = jnp.arange(count)

    def named(sizes, rotation):
        used = int((sizes > 0).sum())
        fixed = max(1, used // 4)
        passed = fixed + (places - fixed + rotation * (used - fixed)) % max(1, count - fixed)
        return jnp.zeros((count,), jnp.int32).at[order[jnp.where(places < fixed, places, passed)]].set(jnp.asarray(sizes, jnp.int32))

    sizes = jnp.where(number % 4 == 0, named(crowded, number // 4), named(ordinary, number - number // 4 - 1))
    mixed = jax.random.permutation(jax.random.fold_in(own, 3), count)
    source_of, receiver = mixed[0:count // 2 * 2:2], mixed[1:count // 2 * 2:2]
    room = jnp.minimum(sizes[source_of] - 1, reach - sizes[receiver]) // 2
    room = jnp.where((source_of == order[0]) | (receiver == order[0]) | (sizes[receiver] == 0), 0, jnp.maximum(room, 0))
    passed = jax.random.randint(jax.random.fold_in(own, 4), (count // 2,), 0, 1 << 20) % (room + 1)
    sizes = sizes.at[source_of].add(-passed).at[receiver].add(passed)
    members = jnp.searchsorted(jnp.cumsum(sizes), jnp.arange(rows * top), side="right").astype(jnp.int32)
    table = members.reshape(top, rows).T
    table = table[jax.random.permutation(jax.random.fold_in(own, 1), rows)]
    rotation = jax.random.randint(jax.random.fold_in(own, 2), (rows, 1), 0, top)
    return jnp.take_along_axis(table, (jnp.arange(top)[None, :] + rotation) % top, axis=1)


def shares(number_of, total, bound, skew, full):
    weights = [(1 << 20) // math.isqrt(grade ** skew) + 1 for grade in range(1, number_of + 1)]
    largest = bound if full else min(bound, max(-(-total // number_of), total * weights[0] // sum(weights)))
    least = 1 if total - largest >= number_of - 1 else 0
    holding, surplus = [largest] + [least] * (number_of - 1), total - largest - least * (number_of - 1)
    while surplus > 0:
        candidates = [i for i in range(1, number_of) if holding[i] < largest] or [i for i in range(1, number_of) if holding[i] < bound]
        pool, left = sum([weights[i] for i in candidates]), surplus
        for i in candidates:
            more = min(bound - holding[i], max(1, left * weights[i] // pool), surplus)
            holding[i] = holding[i] + more
            surplus = surplus - more
    return np.array(holding)


def scatter_about(rng, shape, spread, limit, shards=(), kind=jnp.bfloat16):
    entries = jax.random.normal(rng, shape, jnp.float32) * spread
    if len(shards) > 0:
        entries = levels(rng, shape, shards, -0.22, 0.18) * entries
    return jnp.clip(entries, min=-limit, max=limit).astype(kind)


def setup_inputs(seed: int = 0) -> dict:
    key_of = jax.random.split(jax.random.key(seed), 7)
    tokens = scatter_about(key_of[0], (MB, TOKENS, D), 1.0, 6.0, ((1, 64),))
    routes_keys = jax.random.split(jax.random.fold_in(key_of[1], 1), MB * TOKENS // TOK_DEV)
    routes_turns = jax.random.permutation(jax.random.fold_in(key_of[1], 3), MB * TOKENS // TOK_DEV)
    routes = jax.vmap(lambda own, number: shared_out(jax.random.fold_in(key_of[1], 2), own, number, TOK_DEV, EXPERTS, 2, CAP, 2))(routes_keys, routes_turns).reshape((MB, TOKENS, 2))
    router = scatter_about(key_of[2], (D, EXPERTS), D ** -0.5, 0.109375)
    gate_weight = scatter_about(key_of[3], (EXPERTS, FW, D), D ** -0.5, 0.109375, ((0, 4), (1, 64)))
    up_weight = scatter_about(key_of[4], (EXPERTS, FW, D), D ** -0.5, 0.109375, ((0, 4), (1, 64)))
    down_weight = scatter_about(key_of[5], (EXPERTS, FW, D), FW ** -0.5, 0.0625, ((0, 4), (1, 64)))
    return {"tokens": tokens, "routes": routes, "router": router, "gate_weight": gate_weight, "up_weight": up_weight, "down_weight": down_weight}


def route_targets(route_ids, experts, capacity):
    onehot = (route_ids[:, :, None] == jnp.arange(experts, dtype=jnp.int32)[None, None, :]).astype(jnp.int32)
    flattened = onehot.reshape(-1, experts)
    before = jnp.cumsum(flattened, axis=0) - flattened
    slot_rank = jnp.sum(before * flattened, axis=1).reshape(route_ids.shape)
    return (route_ids * capacity + slot_rank).astype(jnp.int32)


def expert_pass(operands):
    inputs, gate_w, up_w, down_w = operands
    as_float = inputs.astype(jnp.float32)
    gate_part = lax.dot_general(as_float, gate_w.astype(jnp.float32), (((1,), (1,)), ((), ())))
    up_part = lax.dot_general(as_float, up_w.astype(jnp.float32), (((1,), (1,)), ((), ())))
    hidden_units = (jax.nn.silu(gate_part) * up_part).astype(jnp.bfloat16)
    return jnp.dot(hidden_units.astype(jnp.float32), down_w.astype(jnp.float32)).astype(jnp.bfloat16)


def reference(tokens, routes, router, gate_weight, up_weight, down_weight):
    experts = EXPERTS
    capacity = CAP
    groups = N_EXPERT * N_DP
    blocks = MB * groups
    logits = jnp.einsum("mtd,de->mte", tokens.astype(jnp.float32), router.astype(jnp.float32))
    chosen = jnp.take_along_axis(logits, routes, axis=-1)
    logit_gap = chosen[..., 0] - chosen[..., 1]
    first_gate = jax.nn.sigmoid(logit_gap)
    second_gate = jax.nn.sigmoid(-logit_gap)
    hidden_blocks = tokens.reshape(blocks, TOK_DEV, D)
    route_blocks = routes.reshape(blocks, TOK_DEV, 2)
    target = jax.vmap(lambda one_block: route_targets(one_block, experts, capacity))(route_blocks)

    def place(block_rows, block_target):
        buffer_rows = jnp.zeros((experts * capacity, D), jnp.bfloat16)
        buffer_rows = buffer_rows.at[block_target[:, 0]].set(block_rows)
        return buffer_rows.at[block_target[:, 1]].set(block_rows)

    buffers = jax.vmap(place)(hidden_blocks, target)
    per_expert = buffers.reshape(blocks, experts, capacity, D).transpose(1, 0, 2, 3).reshape(experts, blocks * capacity, D)
    results = lax.map(expert_pass, (per_expert, gate_weight, up_weight, down_weight))
    back_rows = results.reshape(experts, blocks, capacity, D).transpose(1, 0, 2, 3).reshape(blocks, experts * capacity, D)
    first_rows = jax.vmap(lambda b_rows, b_target: jnp.take(b_rows, b_target[:, 0], axis=0))(back_rows, target)
    second_rows = jax.vmap(lambda b_rows, b_target: jnp.take(b_rows, b_target[:, 1], axis=0))(back_rows, target)
    first_rows = first_rows.reshape(MB, TOKENS, D).astype(jnp.float32)
    second_rows = second_rows.reshape(MB, TOKENS, D).astype(jnp.float32)
    layer_out = (tokens.astype(jnp.float32) + first_gate[..., None] * first_rows + second_gate[..., None] * second_rows).astype(jnp.bfloat16)

    gram_scale = experts / (2.0 * MB * TOKENS)
    replica_rows = per_expert.reshape(experts, MB, N_EXPERT, N_DP, capacity, D).transpose(0, 3, 1, 2, 4, 5)
    replica_rows = replica_rows.reshape(experts, N_DP, MB * N_EXPERT * capacity, D)

    def gram_pass(rows_of_expert):
        as_float = rows_of_expert.astype(jnp.float32)
        partial_value = (jnp.einsum("nrd,nrf->ndf", as_float, as_float) * gram_scale).astype(jnp.bfloat16)
        partial_value = lax.optimization_barrier(partial_value)
        return jnp.sum(partial_value.astype(jnp.float32), axis=0).astype(jnp.bfloat16)

    grams = lax.map(gram_pass, replica_rows)
    return layer_out, grams
```

```python
import jax
import jax.numpy as jnp
from jax import lax
from jax.sharding import PartitionSpec as P


def route_targets(route_ids, experts, capacity):
    onehot = (route_ids[:, :, None] == jnp.arange(experts, dtype=jnp.int32)[None, None, :]).astype(
        jnp.int32
    )
    flattened = onehot.reshape(-1, experts)
    before = jnp.cumsum(flattened, axis=0) - flattened
    slot_rank = jnp.sum(before * flattened, axis=1).reshape(route_ids.shape)
    return route_ids * capacity + slot_rank


def on_device(tokens, routes, router, gate_weight, up_weight, down_weight):
    micro_count = tokens.shape[0]
    rows_dev = tokens.shape[1]
    model_width = tokens.shape[2]
    experts = router.shape[1]
    capacity = 9 * rows_dev // (4 * experts)
    section_count = lax.axis_size("section")
    replicas = lax.axis_size("dp")
    section_index = lax.axis_index("section")
    dp_index = lax.axis_index("dp")
    col_width = model_width // section_count
    part = capacity // section_count
    logits = jnp.einsum("mtd,de->mte", tokens, router, preferred_element_type=jnp.float32)
    chosen = jnp.take_along_axis(logits, routes, axis=-1)
    logit_gap = chosen[..., 0] - chosen[..., 1]
    first_gate = jax.nn.sigmoid(logit_gap)
    second_gate = jax.nn.sigmoid(-logit_gap)
    target = jax.vmap(lambda one_block: route_targets(one_block, experts, capacity))(routes)
    slot_ids = (
        jnp.arange(experts, dtype=jnp.int32)[:, None] * capacity
        + section_index * part
        + jnp.arange(part, dtype=jnp.int32)[None, :]
    ).reshape(-1)
    placing = jnp.sum(
        (slot_ids[None, :, None, None] == target[:, None, :, :]).astype(jnp.float32), axis=3
    ).astype(jnp.bfloat16)
    outgoing = jnp.einsum(
        "mst,mtd->msd", placing, tokens, preferred_element_type=jnp.float32
    ).astype(jnp.bfloat16)
    outgoing = outgoing.reshape(micro_count, experts, part, model_width)
    arrived = lax.all_to_all(outgoing, "expert", split_axis=1, concat_axis=1, tiled=True)
    rows_all = lax.all_gather(arrived, "dp", axis=0, tiled=False).reshape(-1, model_width)
    gate_piece = lax.all_gather(gate_weight[0], "section", axis=0, tiled=True)
    up_piece = lax.all_gather(up_weight[0], "section", axis=0, tiled=True)
    down_piece = lax.all_gather(down_weight[0], "section", axis=0, tiled=True)
    gate_part = lax.dot_general(
        rows_all, gate_piece, (((1,), (1,)), ((), ())), preferred_element_type=jnp.float32
    )
    up_part = lax.dot_general(
        rows_all, up_piece, (((1,), (1,)), ((), ())), preferred_element_type=jnp.float32
    )
    inner_units = (jax.nn.silu(gate_part) * up_part).astype(jnp.bfloat16)
    partial_out = jnp.dot(inner_units, down_piece, preferred_element_type=jnp.float32)
    summed_out = lax.psum_scatter(
        partial_out.astype(jnp.bfloat16), "dp", scatter_dimension=0, tiled=True
    )
    by_cols = summed_out.reshape(micro_count, experts, part, section_count, col_width)
    by_cols = jnp.moveaxis(by_cols, 3, 0)
    by_parts = lax.all_to_all(by_cols, "section", split_axis=0, concat_axis=0, tiled=True)
    expert_out = jnp.moveaxis(by_parts, 0, 2).reshape(micro_count, experts, capacity, col_width)
    returned = lax.all_to_all(expert_out, "expert", split_axis=1, concat_axis=1, tiled=True)
    flat_back = returned.reshape(micro_count, experts * capacity, col_width)
    first_rows = jnp.take_along_axis(flat_back, target[:, :, 0][:, :, None], axis=1).astype(
        jnp.float32
    )
    second_rows = jnp.take_along_axis(flat_back, target[:, :, 1][:, :, None], axis=1).astype(
        jnp.float32
    )
    own_cols = lax.dynamic_slice_in_dim(tokens, section_index * col_width, col_width, 2).astype(
        jnp.float32
    )
    layer_out = (
        own_cols + first_gate[..., None] * first_rows + second_gate[..., None] * second_rows
    ).astype(jnp.bfloat16)
    all_tokens = rows_dev * lax.axis_size("expert") * replicas
    gram_scale = experts / (2.0 * micro_count * all_tokens)
    block_rows = col_width // replicas
    left_cols = lax.dynamic_slice_in_dim(
        rows_all.reshape(-1, section_count, replicas, block_rows), dp_index, 1, 2
    ).reshape(-1, section_count * block_rows)
    product = (
        lax.dot_general(
            left_cols, rows_all, (((0,), (0,)), ((), ())), preferred_element_type=jnp.float32
        )
        * gram_scale
    )
    gram_block = lax.psum_scatter(
        product.astype(jnp.bfloat16), "section", scatter_dimension=0, tiled=True
    )
    return (layer_out, gram_block[None])


def solution(mesh):
    return jax.shard_map(
        on_device,
        mesh=mesh,
        in_specs=(
            P(None, ("expert", "dp"), None),
            P(None, ("expert", "dp"), None),
            P(),
            P("expert", ("section", "dp"), None),
            P("expert", ("section", "dp"), None),
            P("expert", ("section", "dp"), None),
        ),
        out_specs=(P(None, ("expert", "dp"), "section"), P("expert", ("section", "dp"), None)),
        check_vma=False,
    )
```

```python
import jax
import jax.numpy as jnp
from jax import lax
from jax.sharding import PartitionSpec as P


def route_targets(route_ids, experts, capacity):
    onehot = (route_ids[:, :, None] == jnp.arange(experts, dtype=jnp.int32)[None, None, :]).astype(
        jnp.int32
    )
    flattened = onehot.reshape(-1, experts)
    before = jnp.cumsum(flattened, axis=0) - flattened
    slot_rank = jnp.sum(before * flattened, axis=1).reshape(route_ids.shape)
    return route_ids * capacity + slot_rank


def on_device(tokens, routes, router, gate_weight, up_weight, down_weight):
    micro_count = tokens.shape[0]
    rows_dev = tokens.shape[1]
    model_width = tokens.shape[2]
    experts = router.shape[1]
    capacity = 9 * rows_dev // (4 * experts)
    section_count = lax.axis_size("section")
    replicas = lax.axis_size("dp")
    section_index = lax.axis_index("section")
    dp_index = lax.axis_index("dp")
    col_width = model_width // section_count
    part = capacity // section_count
    logits = jnp.einsum("mtd,de->mte", tokens, router, preferred_element_type=jnp.float32)
    chosen = jnp.take_along_axis(logits, routes, axis=-1)
    logit_gap = chosen[..., 0] - chosen[..., 1]
    first_gate = jax.nn.sigmoid(logit_gap)
    second_gate = jax.nn.sigmoid(-logit_gap)
    target = jax.vmap(lambda one_block: route_targets(one_block, experts, capacity))(routes)
    slot_ids = (
        jnp.arange(experts, dtype=jnp.int32)[:, None] * capacity
        + section_index * part
        + jnp.arange(part, dtype=jnp.int32)[None, :]
    ).reshape(-1)
    placing = jnp.sum(
        (slot_ids[None, :, None, None] == target[:, None, :, :]).astype(jnp.float32), axis=3
    ).astype(jnp.bfloat16)
    outgoing = jnp.einsum(
        "mst,mtd->msd", placing, tokens, preferred_element_type=jnp.float32
    ).astype(jnp.bfloat16)
    outgoing = outgoing.reshape(micro_count, experts, part, model_width)
    arrived = lax.all_to_all(outgoing, "expert", split_axis=1, concat_axis=1, tiled=True)
    copies = jnp.broadcast_to(arrived[None], (replicas,) + arrived.shape)
    rows_all = lax.all_to_all(copies, "dp", split_axis=0, concat_axis=0, tiled=True)
    rows_all = rows_all.reshape(-1, model_width)
    stacked = jnp.stack([gate_weight[0], up_weight[0], down_weight[0]])
    pieces = lax.all_gather(stacked, "section", axis=1, tiled=True)
    gate_piece, up_piece, down_piece = pieces[0], pieces[1], pieces[2]
    gate_part = lax.dot_general(
        rows_all, gate_piece, (((1,), (1,)), ((), ())), preferred_element_type=jnp.float32
    )
    up_part = lax.dot_general(
        rows_all, up_piece, (((1,), (1,)), ((), ())), preferred_element_type=jnp.float32
    )
    inner_units = (jax.nn.silu(gate_part) * up_part).astype(jnp.bfloat16)
    partial_out = jnp.dot(inner_units, down_piece, preferred_element_type=jnp.float32)
    chunks = partial_out.astype(jnp.bfloat16).reshape(replicas, -1, model_width)
    chunks = lax.all_to_all(chunks, "dp", split_axis=0, concat_axis=0, tiled=True)
    summed_out = jnp.sum(chunks.astype(jnp.float32), axis=0).astype(jnp.bfloat16)
    by_cols = summed_out.reshape(micro_count, experts, part, section_count, col_width)
    by_cols = jnp.moveaxis(by_cols, 3, 0)
    by_parts = lax.all_to_all(by_cols, "section", split_axis=0, concat_axis=0, tiled=True)
    expert_out = jnp.moveaxis(by_parts, 0, 2).reshape(micro_count, experts, capacity, col_width)
    returned = lax.all_to_all(expert_out, "expert", split_axis=1, concat_axis=1, tiled=True)
    flat_back = returned.reshape(micro_count, experts * capacity, col_width)
    first_rows = jnp.take_along_axis(flat_back, target[:, :, 0][:, :, None], axis=1).astype(
        jnp.float32
    )
    second_rows = jnp.take_along_axis(flat_back, target[:, :, 1][:, :, None], axis=1).astype(
        jnp.float32
    )
    own_cols = lax.dynamic_slice_in_dim(tokens, section_index * col_width, col_width, 2).astype(
        jnp.float32
    )
    layer_out = (
        own_cols + first_gate[..., None] * first_rows + second_gate[..., None] * second_rows
    ).astype(jnp.bfloat16)
    all_tokens = rows_dev * lax.axis_size("expert") * replicas
    gram_scale = experts / (2.0 * micro_count * all_tokens)
    block_rows = col_width // replicas
    left_cols = lax.dynamic_slice_in_dim(
        rows_all.reshape(-1, section_count, replicas, block_rows), dp_index, 1, 2
    ).reshape(-1, section_count * block_rows)
    product = (
        lax.dot_general(
            left_cols, rows_all, (((0,), (0,)), ((), ())), preferred_element_type=jnp.float32
        )
        * gram_scale
    )
    gram_block = lax.psum_scatter(
        product.astype(jnp.bfloat16), "section", scatter_dimension=0, tiled=True
    )
    return (layer_out, gram_block[None])


def solution(mesh):
    return jax.shard_map(
        on_device,
        mesh=mesh,
        in_specs=(
            P(None, ("expert", "dp"), None),
            P(None, ("expert", "dp"), None),
            P(),
            P("expert", ("section", "dp"), None),
            P("expert", ("section", "dp"), None),
            P("expert", ("section", "dp"), None),
        ),
        out_specs=(P(None, ("expert", "dp"), "section"), P("expert", ("section", "dp"), None)),
        check_vma=False,
    )
```

```python
import jax
import jax.numpy as jnp
from jax import lax
from jax.sharding import PartitionSpec as P


def route_targets(route_ids, experts, capacity):
    onehot = (route_ids[:, :, None] == jnp.arange(experts, dtype=jnp.int32)[None, None, :]).astype(
        jnp.int32
    )
    flattened = onehot.reshape(-1, experts)
    before = jnp.cumsum(flattened, axis=0) - flattened
    slot_rank = jnp.sum(before * flattened, axis=1).reshape(route_ids.shape)
    return route_ids * capacity + slot_rank


def on_device(tokens, routes, router, gate_weight, up_weight, down_weight):
    micro_count = tokens.shape[0]
    rows_dev = tokens.shape[1]
    model_width = tokens.shape[2]
    experts = router.shape[1]
    capacity = 9 * rows_dev // (4 * experts)
    section_count = lax.axis_size("section")
    replicas = lax.axis_size("dp")
    section_index = lax.axis_index("section")
    dp_index = lax.axis_index("dp")
    col_width = model_width // section_count
    part = capacity // section_count
    logits = jnp.einsum("mtd,de->mte", tokens, router, preferred_element_type=jnp.float32)
    chosen = jnp.take_along_axis(logits, routes, axis=-1)
    logit_gap = chosen[..., 0] - chosen[..., 1]
    first_gate = jax.nn.sigmoid(logit_gap)
    second_gate = jax.nn.sigmoid(-logit_gap)
    target = jax.vmap(lambda one_block: route_targets(one_block, experts, capacity))(routes)
    slot_ids = (
        jnp.arange(experts, dtype=jnp.int32)[:, None] * capacity
        + section_index * part
        + jnp.arange(part, dtype=jnp.int32)[None, :]
    ).reshape(-1)
    placing = jnp.sum(
        (slot_ids[None, :, None, None] == target[:, None, :, :]).astype(jnp.float32), axis=3
    ).astype(jnp.bfloat16)
    outgoing = jnp.einsum(
        "mst,mtd->msd", placing, tokens, preferred_element_type=jnp.float32
    ).astype(jnp.bfloat16)
    outgoing = outgoing.reshape(micro_count, experts, part, model_width)
    arrived = lax.all_to_all(outgoing, "expert", split_axis=1, concat_axis=1, tiled=True)
    ring = [2 * p if p < replicas // 2 else 2 * (replicas - 1 - p) + 1 for p in range(replicas)]
    ahead = [(ring[p], ring[(p + 1) % replicas]) for p in range(replicas)]
    behind = [(ring[p], ring[(p - 1) % replicas]) for p in range(replicas)]
    half = replicas // 2
    gathered = [arrived]
    moving = arrived
    for _ in range(half):
        moving = lax.ppermute(moving, "dp", ahead)
        gathered.append(moving)
    moving = arrived
    for _ in range(half - 1):
        moving = lax.ppermute(moving, "dp", behind)
        gathered.append(moving)
    rows_all = jnp.stack(gathered).reshape(-1, model_width)
    stacked = jnp.stack([gate_weight[0], up_weight[0], down_weight[0]])
    pieces = lax.all_gather(stacked, "section", axis=1, tiled=True)
    gate_piece, up_piece, down_piece = pieces[0], pieces[1], pieces[2]
    gate_part = lax.dot_general(
        rows_all, gate_piece, (((1,), (1,)), ((), ())), preferred_element_type=jnp.float32
    )
    up_part = lax.dot_general(
        rows_all, up_piece, (((1,), (1,)), ((), ())), preferred_element_type=jnp.float32
    )
    inner_units = (jax.nn.silu(gate_part) * up_part).astype(jnp.bfloat16)
    partial_out = jnp.dot(inner_units, down_piece, preferred_element_type=jnp.float32)
    chunks = partial_out.reshape(replicas, -1, model_width)
    forward = chunks[half]
    for k in range(1, half + 1):
        if k > 1:
            forward = forward_in.astype(jnp.float32) + chunks[2 * half + 1 - k]
        forward_in = lax.ppermute(forward.astype(jnp.bfloat16), "dp", ahead)
    backward = chunks[half - 1]
    for k in range(1, half):
        if k > 1:
            backward = backward_in.astype(jnp.float32) + chunks[half - k]
        backward_in = lax.ppermute(backward.astype(jnp.bfloat16), "dp", behind)
    summed_out = (
        chunks[0] + forward_in.astype(jnp.float32) + backward_in.astype(jnp.float32)
    ).astype(jnp.bfloat16)
    by_cols = summed_out.reshape(micro_count, experts, part, section_count, col_width)
    by_cols = jnp.moveaxis(by_cols, 3, 0)
    by_parts = lax.all_to_all(by_cols, "section", split_axis=0, concat_axis=0, tiled=True)
    expert_out = jnp.moveaxis(by_parts, 0, 2).reshape(micro_count, experts, capacity, col_width)
    returned = lax.all_to_all(expert_out, "expert", split_axis=1, concat_axis=1, tiled=True)
    flat_back = returned.reshape(micro_count, experts * capacity, col_width)
    first_rows = jnp.take_along_axis(flat_back, target[:, :, 0][:, :, None], axis=1).astype(
        jnp.float32
    )
    second_rows = jnp.take_along_axis(flat_back, target[:, :, 1][:, :, None], axis=1).astype(
        jnp.float32
    )
    own_cols = lax.dynamic_slice_in_dim(tokens, section_index * col_width, col_width, 2).astype(
        jnp.float32
    )
    layer_out = (
        own_cols + first_gate[..., None] * first_rows + second_gate[..., None] * second_rows
    ).astype(jnp.bfloat16)
    all_tokens = rows_dev * lax.axis_size("expert") * replicas
    gram_scale = experts / (2.0 * micro_count * all_tokens)
    block_rows = col_width // replicas
    left_cols = lax.dynamic_slice_in_dim(
        rows_all.reshape(-1, section_count, replicas, block_rows), dp_index, 1, 2
    ).reshape(-1, section_count * block_rows)
    product = (
        lax.dot_general(
            left_cols, rows_all, (((0,), (0,)), ((), ())), preferred_element_type=jnp.float32
        )
        * gram_scale
    )
    gram_block = lax.psum_scatter(
        product.astype(jnp.bfloat16), "section", scatter_dimension=0, tiled=True
    )
    return (layer_out, gram_block[None])


def solution(mesh):
    return jax.shard_map(
        on_device,
        mesh=mesh,
        in_specs=(
            P(None, ("expert", "dp"), None),
            P(None, ("expert", "dp"), None),
            P(),
            P("expert", ("section", "dp"), None),
            P("expert", ("section", "dp"), None),
            P("expert", ("section", "dp"), None),
        ),
        out_specs=(P(None, ("expert", "dp"), "section"), P("expert", ("section", "dp"), None)),
        check_vma=False,
    )
```

```python
import jax
import jax.numpy as jnp
from jax import lax
from jax.sharding import PartitionSpec as P


def route_targets(route_ids, experts, capacity):
    onehot = (route_ids[:, :, None] == jnp.arange(experts, dtype=jnp.int32)[None, None, :]).astype(
        jnp.int32
    )
    flattened = onehot.reshape(-1, experts)
    before = jnp.cumsum(flattened, axis=0) - flattened
    slot_rank = jnp.sum(before * flattened, axis=1).reshape(route_ids.shape)
    return route_ids * capacity + slot_rank


def on_device(tokens, routes, router, gate_weight, up_weight, down_weight):
    micro_count = tokens.shape[0]
    rows_dev = tokens.shape[1]
    model_width = tokens.shape[2]
    experts = router.shape[1]
    capacity = 9 * rows_dev // (4 * experts)
    section_count = lax.axis_size("section")
    replicas = lax.axis_size("dp")
    section_index = lax.axis_index("section")
    dp_index = lax.axis_index("dp")
    col_width = model_width // section_count
    part = capacity // section_count
    logits = jnp.einsum("mtd,de->mte", tokens, router, preferred_element_type=jnp.float32)
    chosen = jnp.take_along_axis(logits, routes, axis=-1)
    logit_gap = chosen[..., 0] - chosen[..., 1]
    first_gate = jax.nn.sigmoid(logit_gap)
    second_gate = jax.nn.sigmoid(-logit_gap)
    target = jax.vmap(lambda one_block: route_targets(one_block, experts, capacity))(routes)
    slot_ids = (
        jnp.arange(experts, dtype=jnp.int32)[:, None] * capacity
        + section_index * part
        + jnp.arange(part, dtype=jnp.int32)[None, :]
    ).reshape(-1)
    placing = jnp.sum(
        (slot_ids[None, :, None, None] == target[:, None, :, :]).astype(jnp.float32), axis=3
    ).astype(jnp.bfloat16)
    outgoing = jnp.einsum(
        "mst,mtd->msd", placing, tokens, preferred_element_type=jnp.float32
    ).astype(jnp.bfloat16)
    outgoing = outgoing.reshape(micro_count, experts, part, model_width)
    arrived = lax.all_to_all(outgoing, "expert", split_axis=1, concat_axis=1, tiled=True)
    own_chunk = arrived.reshape(-1, model_width)
    block_rows = col_width // replicas
    gram_cols = (
        jnp.arange(section_count, dtype=jnp.int32)[:, None] * col_width
        + dp_index * block_rows
        + jnp.arange(block_rows, dtype=jnp.int32)[None, :]
    ).reshape(-1)
    picker = (jnp.arange(model_width, dtype=jnp.int32)[:, None] == gram_cols[None, :]).astype(
        jnp.bfloat16
    )

    def gram_of(chunk):
        left = jnp.dot(chunk, picker, preferred_element_type=jnp.float32).astype(jnp.bfloat16)
        return lax.dot_general(
            left, chunk, (((0,), (0,)), ((), ())), preferred_element_type=jnp.float32
        )

    ring = [2 * p if p < replicas // 2 else 2 * (replicas - 1 - p) + 1 for p in range(replicas)]
    ahead = [(ring[p], ring[(p + 1) % replicas]) for p in range(replicas)]
    behind = [(ring[p], ring[(p - 1) % replicas]) for p in range(replicas)]
    half = replicas // 2

    def ring_gather(perm, steps, acc):
        got, pending = [], []
        moving = own_chunk
        for _ in range(steps):
            if len(pending) >= 2:
                contrib = gram_of(pending.pop(0))
                acc = contrib if acc is None else acc + contrib
                moving, acc = lax.optimization_barrier((moving, acc))
            moving = lax.ppermute(moving, "dp", perm)
            got.append(moving)
            pending.append(moving)
        for chunk in pending:
            contrib = gram_of(chunk)
            acc = contrib if acc is None else acc + contrib
        return got, acc

    from_behind, gram_behind = ring_gather(ahead, half, gram_of(own_chunk))
    from_ahead, gram_ahead = ring_gather(behind, half - 1, None)
    gram_acc = gram_behind + gram_ahead
    rows_all = jnp.concatenate([own_chunk] + from_behind + from_ahead, axis=0)
    stacked = jnp.stack([gate_weight[0], up_weight[0], down_weight[0]])
    pieces = lax.all_gather(stacked, "section", axis=1, tiled=True)
    gate_piece, up_piece, down_piece = pieces[0], pieces[1], pieces[2]
    gate_part = lax.dot_general(
        rows_all, gate_piece, (((1,), (1,)), ((), ())), preferred_element_type=jnp.float32
    )
    up_part = lax.dot_general(
        rows_all, up_piece, (((1,), (1,)), ((), ())), preferred_element_type=jnp.float32
    )
    inner_units = (jax.nn.silu(gate_part) * up_part).astype(jnp.bfloat16)
    partial_out = jnp.dot(inner_units, down_piece, preferred_element_type=jnp.float32)
    chunks = partial_out.reshape(replicas, -1, model_width)
    forward = chunks[half]
    for k in range(1, half + 1):
        if k > 1:
            forward = forward_in.astype(jnp.float32) + chunks[2 * half + 1 - k]
        forward_in = lax.ppermute(forward.astype(jnp.bfloat16), "dp", ahead)
    backward = chunks[half - 1]
    for k in range(1, half):
        if k > 1:
            backward = backward_in.astype(jnp.float32) + chunks[half - k]
        backward_in = lax.ppermute(backward.astype(jnp.bfloat16), "dp", behind)
    summed_out = (
        chunks[0] + forward_in.astype(jnp.float32) + backward_in.astype(jnp.float32)
    ).astype(jnp.bfloat16)
    by_cols = summed_out.reshape(micro_count, experts, part, section_count, col_width)
    by_cols = jnp.moveaxis(by_cols, 3, 0)
    by_parts = lax.all_to_all(by_cols, "section", split_axis=0, concat_axis=0, tiled=True)
    expert_out = jnp.moveaxis(by_parts, 0, 2).reshape(micro_count, experts, capacity, col_width)
    returned = lax.all_to_all(expert_out, "expert", split_axis=1, concat_axis=1, tiled=True)
    flat_back = returned.reshape(micro_count, experts * capacity, col_width)
    first_rows = jnp.take_along_axis(flat_back, target[:, :, 0][:, :, None], axis=1).astype(
        jnp.float32
    )
    second_rows = jnp.take_along_axis(flat_back, target[:, :, 1][:, :, None], axis=1).astype(
        jnp.float32
    )
    own_cols = lax.dynamic_slice_in_dim(tokens, section_index * col_width, col_width, 2).astype(
        jnp.float32
    )
    layer_out = (
        own_cols + first_gate[..., None] * first_rows + second_gate[..., None] * second_rows
    ).astype(jnp.bfloat16)
    all_tokens = rows_dev * lax.axis_size("expert") * replicas
    gram_scale = experts / (2.0 * micro_count * all_tokens)
    product = gram_acc * gram_scale
    gram_block = lax.psum_scatter(
        product.astype(jnp.bfloat16), "section", scatter_dimension=0, tiled=True
    )
    return (layer_out, gram_block[None])


def solution(mesh):
    return jax.shard_map(
        on_device,
        mesh=mesh,
        in_specs=(
            P(None, ("expert", "dp"), None),
            P(None, ("expert", "dp"), None),
            P(),
            P("expert", ("section", "dp"), None),
            P("expert", ("section", "dp"), None),
            P("expert", ("section", "dp"), None),
        ),
        out_specs=(P(None, ("expert", "dp"), "section"), P("expert", ("section", "dp"), None)),
        check_vma=False,
    )
```

```python
import jax
import jax.numpy as jnp
from jax import lax
from jax.sharding import Mesh
from jax.sharding import PartitionSpec as P


def route_targets(route_ids, experts, capacity):
    onehot = (route_ids[:, :, None] == jnp.arange(experts, dtype=jnp.int32)[None, None, :]).astype(
        jnp.int32
    )
    flattened = onehot.reshape(-1, experts)
    before = jnp.cumsum(flattened, axis=0) - flattened
    slot_rank = jnp.sum(before * flattened, axis=1).reshape(route_ids.shape)
    return route_ids * capacity + slot_rank


def ring_pairs(count, step):
    return [(i, (i + step) % count) for i in range(count)]


def on_device(tokens, routes, router, gate_weight, up_weight, down_weight):
    micro_count = tokens.shape[0]
    rows_dev = tokens.shape[1]
    model_width = tokens.shape[2]
    experts = router.shape[1]
    capacity = 9 * rows_dev // (4 * experts)
    hi_count = lax.axis_size("xh")
    core_count = lax.axis_size("c")
    z_count = lax.axis_size("z")
    lo_count = lax.axis_size("xl")
    section_count = hi_count * core_count
    replicas = z_count * lo_count
    hi_index = lax.axis_index("xh")
    core_index = lax.axis_index("c")
    z_index = lax.axis_index("z")
    lo_index = lax.axis_index("xl")
    section_index = hi_index * core_count + core_index
    col_width = model_width // section_count
    part = capacity // core_count
    logits = jnp.einsum("mtd,de->mte", tokens, router, preferred_element_type=jnp.float32)
    chosen = jnp.take_along_axis(logits, routes, axis=-1)
    logit_gap = chosen[..., 0] - chosen[..., 1]
    first_gate = jax.nn.sigmoid(logit_gap)
    second_gate = jax.nn.sigmoid(-logit_gap)
    target = jax.vmap(lambda one_block: route_targets(one_block, experts, capacity))(routes)
    slot_ids = (
        jnp.arange(experts, dtype=jnp.int32)[:, None] * capacity
        + core_index * part
        + jnp.arange(part, dtype=jnp.int32)[None, :]
    ).reshape(-1)
    placing = jnp.sum(
        (slot_ids[None, :, None, None] == target[:, None, :, :]).astype(jnp.float32), axis=3
    ).astype(jnp.bfloat16)
    outgoing = jnp.einsum(
        "mst,mtd->msd", placing, tokens, preferred_element_type=jnp.float32
    ).astype(jnp.bfloat16)
    outgoing = outgoing.reshape(micro_count, experts, part, model_width)
    arrived = lax.all_to_all(outgoing, "expert", split_axis=1, concat_axis=1, tiled=True)
    own_chunk = arrived.reshape(-1, model_width)
    stacked = jnp.stack([gate_weight[0], up_weight[0], down_weight[0]])
    pieces = lax.all_gather(stacked, ("c", "xl"), axis=1, tiled=True)
    gate_piece, up_piece, down_piece = pieces[0], pieces[1], pieces[2]
    half = z_count // 2
    ahead = ring_pairs(z_count, 1)
    behind = ring_pairs(z_count, -1)
    gathered = [own_chunk]
    moving = own_chunk
    for _ in range(half):
        moving = lax.ppermute(moving, "z", ahead)
        gathered.append(moving)
    moving = own_chunk
    for _ in range(half - 1):
        moving = lax.ppermute(moving, "z", behind)
        gathered.append(moving)
    rows_all = jnp.concatenate(gathered, axis=0)
    gate_part = lax.dot_general(
        rows_all, gate_piece, (((1,), (1,)), ((), ())), preferred_element_type=jnp.float32
    )
    up_part = lax.dot_general(
        rows_all, up_piece, (((1,), (1,)), ((), ())), preferred_element_type=jnp.float32
    )
    inner_units = (jax.nn.silu(gate_part) * up_part).astype(jnp.bfloat16)
    partial_out = jnp.dot(inner_units, down_piece, preferred_element_type=jnp.float32)
    chunks = partial_out.reshape(z_count, -1, model_width)
    forward = chunks[half]
    for k in range(1, half + 1):
        if k > 1:
            forward = forward_in.astype(jnp.float32) + chunks[2 * half + 1 - k]
        forward_in = lax.ppermute(forward.astype(jnp.bfloat16), "z", ahead)
    backward = chunks[half - 1]
    for k in range(1, half):
        if k > 1:
            backward = backward_in.astype(jnp.float32) + chunks[half - k]
        backward_in = lax.ppermute(backward.astype(jnp.bfloat16), "z", behind)
    summed = chunks[0] + forward_in.astype(jnp.float32) + backward_in.astype(jnp.float32)
    halves = summed.reshape(-1, hi_count, col_width * core_count)
    other = lax.dynamic_index_in_dim(halves, 1 - hi_index, 1, keepdims=False)
    mine = lax.dynamic_index_in_dim(halves, hi_index, 1, keepdims=False)
    swapped = lax.ppermute(other.astype(jnp.bfloat16), "xh", ring_pairs(hi_count, 1))
    own_half = (mine + swapped.astype(jnp.float32)).astype(jnp.bfloat16)
    by_cols = jnp.moveaxis(own_half.reshape(-1, core_count, col_width), 1, 0)
    by_parts = lax.all_to_all(by_cols, "c", split_axis=0, concat_axis=0, tiled=True)
    by_parts = by_parts.reshape(core_count, micro_count, experts, part, col_width)
    expert_out = jnp.moveaxis(by_parts, 0, 2).reshape(micro_count, experts, capacity, col_width)
    returned = lax.all_to_all(expert_out, "expert", split_axis=1, concat_axis=1, tiled=True)
    flat_back = returned.reshape(micro_count, experts * capacity, col_width)
    first_rows = jnp.take_along_axis(flat_back, target[:, :, 0][:, :, None], axis=1).astype(
        jnp.float32
    )
    second_rows = jnp.take_along_axis(flat_back, target[:, :, 1][:, :, None], axis=1).astype(
        jnp.float32
    )
    own_cols = lax.dynamic_slice_in_dim(tokens, section_index * col_width, col_width, 2).astype(
        jnp.float32
    )
    layer_out = (
        own_cols + first_gate[..., None] * first_rows + second_gate[..., None] * second_rows
    ).astype(jnp.bfloat16)
    all_tokens = rows_dev * lax.axis_size("expert") * replicas
    gram_scale = experts / (2.0 * micro_count * all_tokens)
    block_rows = col_width // replicas
    pool_core = jnp.arange(core_count, dtype=jnp.int32)[:, None, None]
    pool_lo = jnp.arange(lo_count, dtype=jnp.int32)[None, :, None]
    gram_cols = (
        (hi_index * core_count + pool_core) * col_width
        + (z_index * lo_count + pool_lo) * block_rows
        + jnp.arange(block_rows, dtype=jnp.int32)[None, None, :]
    ).reshape(-1)
    picker = (jnp.arange(model_width, dtype=jnp.int32)[:, None] == gram_cols[None, :]).astype(
        jnp.bfloat16
    )
    left = jnp.dot(rows_all, picker, preferred_element_type=jnp.float32).astype(jnp.bfloat16)
    product = (
        lax.dot_general(left, rows_all, (((0,), (0,)), ((), ())), preferred_element_type=jnp.float32)
        * gram_scale
    )
    gram_block = lax.psum_scatter(
        product.astype(jnp.bfloat16), ("c", "xl"), scatter_dimension=0, tiled=True
    )
    return (layer_out, gram_block[None])


def solution(mesh):
    section, expert, dp = mesh.devices.shape
    fine = Mesh(
        mesh.devices.reshape(2, section // 2, expert, dp // 2, 2), ("xh", "c", "expert", "z", "xl")
    )
    tokens_spec = P(None, ("expert", "z", "xl"), None)
    weight_spec = P("expert", ("xh", "c", "z", "xl"), None)
    return jax.shard_map(
        on_device,
        mesh=fine,
        in_specs=(tokens_spec, tokens_spec, P(), weight_spec, weight_spec, weight_spec),
        out_specs=(P(None, ("expert", "z", "xl"), ("xh", "c")), weight_spec),
        check_vma=False,
    )
```

```python
import jax
import jax.numpy as jnp
from jax import lax
from jax.sharding import Mesh
from jax.sharding import PartitionSpec as P


def route_targets(route_ids, experts, capacity):
    onehot = (route_ids[:, :, None] == jnp.arange(experts, dtype=jnp.int32)[None, None, :]).astype(
        jnp.int32
    )
    flattened = onehot.reshape(-1, experts)
    before = jnp.cumsum(flattened, axis=0) - flattened
    slot_rank = jnp.sum(before * flattened, axis=1).reshape(route_ids.shape)
    return route_ids * capacity + slot_rank


def ring_pairs(count, step):
    return [(i, (i + step) % count) for i in range(count)]


def on_device(tokens, routes, router, gate_weight, up_weight, down_weight):
    micro_count = tokens.shape[0]
    rows_dev = tokens.shape[1]
    model_width = tokens.shape[2]
    experts = router.shape[1]
    capacity = 9 * rows_dev // (4 * experts)
    hi_count = lax.axis_size("xh")
    core_count = lax.axis_size("c")
    z_count = lax.axis_size("z")
    lo_count = lax.axis_size("xl")
    section_count = hi_count * core_count
    replicas = z_count * lo_count
    hi_index = lax.axis_index("xh")
    core_index = lax.axis_index("c")
    z_index = lax.axis_index("z")
    lo_index = lax.axis_index("xl")
    section_index = hi_index * core_count + core_index
    col_width = model_width // section_count
    part = capacity // core_count
    logits = jnp.einsum("mtd,de->mte", tokens, router, preferred_element_type=jnp.float32)
    chosen = jnp.take_along_axis(logits, routes, axis=-1)
    logit_gap = chosen[..., 0] - chosen[..., 1]
    first_gate = jax.nn.sigmoid(logit_gap)
    second_gate = jax.nn.sigmoid(-logit_gap)
    target = jax.vmap(lambda one_block: route_targets(one_block, experts, capacity))(routes)
    slot_ids = (
        jnp.arange(experts, dtype=jnp.int32)[:, None] * capacity
        + core_index * part
        + jnp.arange(part, dtype=jnp.int32)[None, :]
    ).reshape(-1)
    placing = jnp.sum(
        (slot_ids[None, :, None, None] == target[:, None, :, :]).astype(jnp.float32), axis=3
    ).astype(jnp.bfloat16)
    outgoing = jnp.einsum(
        "mst,mtd->msd", placing, tokens, preferred_element_type=jnp.float32
    ).astype(jnp.bfloat16)
    outgoing = outgoing.reshape(micro_count, experts, part, model_width)
    arrived = lax.all_to_all(outgoing, "expert", split_axis=1, concat_axis=1, tiled=True)
    own_chunk = arrived.reshape(-1, model_width)
    stacked = jnp.stack([gate_weight[0], up_weight[0], down_weight[0]])
    from_lo = lax.ppermute(stacked, "xl", ring_pairs(lo_count, 1))
    pair = jnp.concatenate([stacked, from_lo], axis=1)
    from_core = lax.ppermute(pair, "c", ring_pairs(core_count, 1))
    pieces = jnp.concatenate([pair, from_core], axis=1)
    gate_piece, up_piece, down_piece = pieces[0], pieces[1], pieces[2]
    half = z_count // 2
    ahead = ring_pairs(z_count, 1)
    behind = ring_pairs(z_count, -1)
    gathered = [own_chunk]
    moving = own_chunk
    for _ in range(half):
        moving = lax.ppermute(moving, "z", ahead)
        gathered.append(moving)
    moving = own_chunk
    for _ in range(half - 1):
        moving = lax.ppermute(moving, "z", behind)
        gathered.append(moving)
    rows_all = jnp.concatenate(gathered, axis=0)
    gate_part = lax.dot_general(
        rows_all, gate_piece, (((1,), (1,)), ((), ())), preferred_element_type=jnp.float32
    )
    up_part = lax.dot_general(
        rows_all, up_piece, (((1,), (1,)), ((), ())), preferred_element_type=jnp.float32
    )
    inner_units = (jax.nn.silu(gate_part) * up_part).astype(jnp.bfloat16)
    partial_out = jnp.dot(inner_units, down_piece, preferred_element_type=jnp.float32)
    chunks = partial_out.reshape(z_count, -1, model_width)
    forward = chunks[half]
    for k in range(1, half + 1):
        if k > 1:
            forward = forward_in.astype(jnp.float32) + chunks[2 * half + 1 - k]
        forward_in = lax.ppermute(forward.astype(jnp.bfloat16), "z", ahead)
    backward = chunks[half - 1]
    for k in range(1, half):
        if k > 1:
            backward = backward_in.astype(jnp.float32) + chunks[half - k]
        backward_in = lax.ppermute(backward.astype(jnp.bfloat16), "z", behind)
    summed = chunks[0] + forward_in.astype(jnp.float32) + backward_in.astype(jnp.float32)
    halves = summed.reshape(-1, hi_count, col_width * core_count)
    other = lax.dynamic_index_in_dim(halves, 1 - hi_index, 1, keepdims=False)
    mine = lax.dynamic_index_in_dim(halves, hi_index, 1, keepdims=False)
    swapped = lax.ppermute(other.astype(jnp.bfloat16), "xh", ring_pairs(hi_count, 1))
    own_half = (mine + swapped.astype(jnp.float32)).astype(jnp.bfloat16)
    by_cols = jnp.moveaxis(own_half.reshape(-1, core_count, col_width), 1, 0)
    by_parts = lax.all_to_all(by_cols, "c", split_axis=0, concat_axis=0, tiled=True)
    by_parts = by_parts.reshape(core_count, micro_count, experts, part, col_width)
    expert_out = jnp.moveaxis(by_parts, 0, 2).reshape(micro_count, experts, capacity, col_width)
    returned = lax.all_to_all(expert_out, "expert", split_axis=1, concat_axis=1, tiled=True)
    flat_back = returned.reshape(micro_count, experts * capacity, col_width)
    first_rows = jnp.take_along_axis(flat_back, target[:, :, 0][:, :, None], axis=1).astype(
        jnp.float32
    )
    second_rows = jnp.take_along_axis(flat_back, target[:, :, 1][:, :, None], axis=1).astype(
        jnp.float32
    )
    own_cols = lax.dynamic_slice_in_dim(tokens, section_index * col_width, col_width, 2).astype(
        jnp.float32
    )
    layer_out = (
        own_cols + first_gate[..., None] * first_rows + second_gate[..., None] * second_rows
    ).astype(jnp.bfloat16)
    all_tokens = rows_dev * lax.axis_size("expert") * replicas
    gram_scale = experts / (2.0 * micro_count * all_tokens)
    block_rows = col_width // replicas
    pool_core = jnp.arange(core_count, dtype=jnp.int32)[:, None, None]
    pool_lo = jnp.arange(lo_count, dtype=jnp.int32)[None, :, None]
    gram_cols = (
        (hi_index * core_count + pool_core) * col_width
        + (z_index * lo_count + pool_lo) * block_rows
        + jnp.arange(block_rows, dtype=jnp.int32)[None, None, :]
    ).reshape(-1)
    picker = (jnp.arange(model_width, dtype=jnp.int32)[:, None] == gram_cols[None, :]).astype(
        jnp.bfloat16
    )
    left = jnp.dot(rows_all, picker, preferred_element_type=jnp.float32).astype(jnp.bfloat16)
    product = (
        lax.dot_general(left, rows_all, (((0,), (0,)), ((), ())), preferred_element_type=jnp.float32)
        * gram_scale
    )
    gram_block = lax.psum_scatter(
        product.astype(jnp.bfloat16), ("c", "xl"), scatter_dimension=0, tiled=True
    )
    return (layer_out, gram_block[None])


def solution(mesh):
    section, expert, dp = mesh.devices.shape
    fine = Mesh(
        mesh.devices.reshape(2, section // 2, expert, dp // 2, 2), ("xh", "c", "expert", "z", "xl")
    )
    tokens_spec = P(None, ("expert", "z", "xl"), None)
    weight_spec = P("expert", ("xh", "c", "z", "xl"), None)
    return jax.shard_map(
        on_device,
        mesh=fine,
        in_specs=(tokens_spec, tokens_spec, P(), weight_spec, weight_spec, weight_spec),
        out_specs=(P(None, ("expert", "z", "xl"), ("xh", "c")), weight_spec),
        check_vma=False,
    )
```

```python
import jax
import jax.numpy as jnp
from jax import lax
from jax.sharding import Mesh
from jax.sharding import PartitionSpec as P


def route_targets(route_ids, experts, capacity):
    onehot = (route_ids[:, :, None] == jnp.arange(experts, dtype=jnp.int32)[None, None, :]).astype(
        jnp.int32
    )
    flattened = onehot.reshape(-1, experts)
    before = jnp.cumsum(flattened, axis=0) - flattened
    slot_rank = jnp.sum(before * flattened, axis=1).reshape(route_ids.shape)
    return route_ids * capacity + slot_rank


def ring_pairs(count, step):
    return [(i, (i + step) % count) for i in range(count)]


def on_device(tokens, routes, router, gate_weight, up_weight, down_weight):
    micro_count = tokens.shape[0]
    rows_dev = tokens.shape[1]
    model_width = tokens.shape[2]
    experts = router.shape[1]
    capacity = 9 * rows_dev // (4 * experts)
    hi_count = lax.axis_size("xh")
    core_count = lax.axis_size("c")
    z_count = lax.axis_size("z")
    lo_count = lax.axis_size("xl")
    section_count = hi_count * core_count
    replicas = z_count * lo_count
    hi_index = lax.axis_index("xh")
    core_index = lax.axis_index("c")
    z_index = lax.axis_index("z")
    lo_index = lax.axis_index("xl")
    section_index = hi_index * core_count + core_index
    col_width = model_width // section_count
    part = capacity // core_count
    logits = jnp.einsum("mtd,de->mte", tokens, router, preferred_element_type=jnp.float32)
    chosen = jnp.take_along_axis(logits, routes, axis=-1)
    logit_gap = chosen[..., 0] - chosen[..., 1]
    first_gate = jax.nn.sigmoid(logit_gap)
    second_gate = jax.nn.sigmoid(-logit_gap)
    target = jax.vmap(lambda one_block: route_targets(one_block, experts, capacity))(routes)
    slot_ids = (
        jnp.arange(experts, dtype=jnp.int32)[:, None] * capacity
        + core_index * part
        + jnp.arange(part, dtype=jnp.int32)[None, :]
    ).reshape(-1)
    placing = jnp.sum(
        (slot_ids[None, :, None, None] == target[:, None, :, :]).astype(jnp.float32), axis=3
    ).astype(jnp.bfloat16)
    outgoing = jnp.einsum(
        "mst,mtd->msd", placing, tokens, preferred_element_type=jnp.float32
    ).astype(jnp.bfloat16)
    outgoing = outgoing.reshape(micro_count, experts, part, model_width)
    arrived = lax.all_to_all(outgoing, "expert", split_axis=1, concat_axis=1, tiled=True)
    own_chunk = arrived.reshape(-1, model_width)
    stacked = jnp.stack([gate_weight[0], up_weight[0], down_weight[0]])
    from_lo = lax.ppermute(stacked, "xl", ring_pairs(lo_count, 1))
    pair = jnp.concatenate([stacked, from_lo], axis=1)
    half = z_count // 2
    ahead = ring_pairs(z_count, 1)
    behind = ring_pairs(z_count, -1)
    from_behind, from_ahead = [], []
    moving_ahead = own_chunk
    moving_behind = own_chunk
    for step in range(half):
        moving_ahead = lax.ppermute(moving_ahead, "z", ahead)
        from_behind.append(moving_ahead)
        if step < half - 1:
            moving_behind = lax.ppermute(moving_behind, "z", behind)
            from_ahead.append(moving_behind)
        if step == 1:
            moving_ahead, moving_behind, pair = lax.optimization_barrier(
                (moving_ahead, moving_behind, pair)
            )
    from_core = lax.ppermute(pair, "c", ring_pairs(core_count, 1))
    pieces = jnp.concatenate([pair, from_core], axis=1)
    gate_piece, up_piece, down_piece = pieces[0], pieces[1], pieces[2]
    gathered = [own_chunk] + from_behind + from_ahead
    rows_all = jnp.concatenate(gathered, axis=0)
    gate_part = lax.dot_general(
        rows_all, gate_piece, (((1,), (1,)), ((), ())), preferred_element_type=jnp.float32
    )
    up_part = lax.dot_general(
        rows_all, up_piece, (((1,), (1,)), ((), ())), preferred_element_type=jnp.float32
    )
    inner_units = (jax.nn.silu(gate_part) * up_part).astype(jnp.bfloat16)
    partial_out = jnp.dot(inner_units, down_piece, preferred_element_type=jnp.float32)
    all_tokens = rows_dev * lax.axis_size("expert") * replicas
    gram_scale = experts / (2.0 * micro_count * all_tokens)
    block_rows = col_width // replicas
    pool_core = jnp.arange(core_count, dtype=jnp.int32)[:, None, None]
    pool_lo = jnp.arange(lo_count, dtype=jnp.int32)[None, :, None]
    gram_cols = (
        (hi_index * core_count + pool_core) * col_width
        + (z_index * lo_count + pool_lo) * block_rows
        + jnp.arange(block_rows, dtype=jnp.int32)[None, None, :]
    ).reshape(-1)
    picker = (jnp.arange(model_width, dtype=jnp.int32)[:, None] == gram_cols[None, :]).astype(
        jnp.bfloat16
    )
    left = jnp.dot(rows_all, picker, preferred_element_type=jnp.float32).astype(jnp.bfloat16)
    product = (
        lax.dot_general(left, rows_all, (((0,), (0,)), ((), ())), preferred_element_type=jnp.float32)
        * gram_scale
    )
    chunks = partial_out.reshape(z_count, -1, model_width)
    forward = chunks[half]
    for k in range(1, half + 1):
        if k > 1:
            forward = forward_in.astype(jnp.float32) + chunks[2 * half + 1 - k]
        if k == 2:
            forward, product = lax.optimization_barrier((forward, product))
        forward_in = lax.ppermute(forward.astype(jnp.bfloat16), "z", ahead)
    backward = chunks[half - 1]
    for k in range(1, half):
        if k > 1:
            backward = backward_in.astype(jnp.float32) + chunks[half - k]
        backward_in = lax.ppermute(backward.astype(jnp.bfloat16), "z", behind)
    summed = chunks[0] + forward_in.astype(jnp.float32) + backward_in.astype(jnp.float32)
    halves = summed.reshape(-1, hi_count, col_width * core_count)
    other = lax.dynamic_index_in_dim(halves, 1 - hi_index, 1, keepdims=False)
    mine = lax.dynamic_index_in_dim(halves, hi_index, 1, keepdims=False)
    swapped = lax.ppermute(other.astype(jnp.bfloat16), "xh", ring_pairs(hi_count, 1))
    own_half = (mine + swapped.astype(jnp.float32)).astype(jnp.bfloat16)
    by_cols = jnp.moveaxis(own_half.reshape(-1, core_count, col_width), 1, 0)
    by_parts = lax.all_to_all(by_cols, "c", split_axis=0, concat_axis=0, tiled=True)
    by_parts = by_parts.reshape(core_count, micro_count, experts, part, col_width)
    expert_out = jnp.moveaxis(by_parts, 0, 2).reshape(micro_count, experts, capacity, col_width)
    returned = lax.all_to_all(expert_out, "expert", split_axis=1, concat_axis=1, tiled=True)
    flat_back = returned.reshape(micro_count, experts * capacity, col_width)
    first_rows = jnp.take_along_axis(flat_back, target[:, :, 0][:, :, None], axis=1).astype(
        jnp.float32
    )
    second_rows = jnp.take_along_axis(flat_back, target[:, :, 1][:, :, None], axis=1).astype(
        jnp.float32
    )
    own_cols = lax.dynamic_slice_in_dim(tokens, section_index * col_width, col_width, 2).astype(
        jnp.float32
    )
    layer_out = (
        own_cols + first_gate[..., None] * first_rows + second_gate[..., None] * second_rows
    ).astype(jnp.bfloat16)
    gram_block = lax.psum_scatter(
        product.astype(jnp.bfloat16), ("c", "xl"), scatter_dimension=0, tiled=True
    )
    return (layer_out, gram_block[None])


def solution(mesh):
    section, expert, dp = mesh.devices.shape
    fine = Mesh(
        mesh.devices.reshape(2, section // 2, expert, dp // 2, 2), ("xh", "c", "expert", "z", "xl")
    )
    tokens_spec = P(None, ("expert", "z", "xl"), None)
    weight_spec = P("expert", ("xh", "c", "z", "xl"), None)
    return jax.shard_map(
        on_device,
        mesh=fine,
        in_specs=(tokens_spec, tokens_spec, P(), weight_spec, weight_spec, weight_spec),
        out_specs=(P(None, ("expert", "z", "xl"), ("xh", "c")), weight_spec),
        check_vma=False,
    )
```

```python
import jax
import jax.numpy as jnp
from jax import lax
from jax.sharding import Mesh
from jax.sharding import PartitionSpec as P


def route_targets(route_ids, experts, capacity):
    onehot = (route_ids[:, :, None] == jnp.arange(experts, dtype=jnp.int32)[None, None, :]).astype(
        jnp.int32
    )
    flattened = onehot.reshape(-1, experts)
    before = jnp.cumsum(flattened, axis=0) - flattened
    slot_rank = jnp.sum(before * flattened, axis=1).reshape(route_ids.shape)
    return route_ids * capacity + slot_rank


def ring_pairs(count, step):
    return [(i, (i + step) % count) for i in range(count)]


def on_device(tokens, routes, router, gate_weight, up_weight, down_weight):
    micro_count = tokens.shape[0]
    rows_dev = tokens.shape[1]
    model_width = tokens.shape[2]
    experts = router.shape[1]
    capacity = 9 * rows_dev // (4 * experts)
    hi_count = lax.axis_size("xh")
    core_count = lax.axis_size("c")
    z_count = lax.axis_size("z")
    lo_count = lax.axis_size("xl")
    section_count = hi_count * core_count
    replicas = z_count * lo_count
    hi_index = lax.axis_index("xh")
    core_index = lax.axis_index("c")
    z_index = lax.axis_index("z")
    lo_index = lax.axis_index("xl")
    section_index = hi_index * core_count + core_index
    col_width = model_width // section_count
    part = capacity // core_count
    logits = jnp.einsum("mtd,de->mte", tokens, router, preferred_element_type=jnp.float32)
    chosen = jnp.take_along_axis(logits, routes, axis=-1)
    logit_gap = chosen[..., 0] - chosen[..., 1]
    first_gate = jax.nn.sigmoid(logit_gap)
    second_gate = jax.nn.sigmoid(-logit_gap)
    target = jax.vmap(lambda one_block: route_targets(one_block, experts, capacity))(routes)
    slot_ids = (
        jnp.arange(experts, dtype=jnp.int32)[:, None] * capacity
        + core_index * part
        + jnp.arange(part, dtype=jnp.int32)[None, :]
    ).reshape(-1)
    placing = jnp.sum(
        (slot_ids[None, :, None, None] == target[:, None, :, :]).astype(jnp.float32), axis=3
    ).astype(jnp.bfloat16)
    outgoing = jnp.einsum(
        "mst,mtd->msd", placing, tokens, preferred_element_type=jnp.float32
    ).astype(jnp.bfloat16)
    outgoing = outgoing.reshape(micro_count, experts, part, model_width)
    arrived = lax.all_to_all(outgoing, "expert", split_axis=1, concat_axis=1, tiled=True)
    own_chunk = arrived.reshape(-1, model_width)
    stacked = jnp.stack([gate_weight[0], up_weight[0], down_weight[0]])
    from_lo = lax.ppermute(stacked, "xl", ring_pairs(lo_count, 1))
    pair = jnp.concatenate([stacked, from_lo], axis=1)
    half = z_count // 2
    ahead = ring_pairs(z_count, 1)
    behind = ring_pairs(z_count, -1)
    from_behind, from_ahead = [], []
    moving_ahead = own_chunk
    moving_behind = own_chunk
    for step in range(half):
        moving_ahead = lax.ppermute(moving_ahead, "z", ahead)
        from_behind.append(moving_ahead)
        if step < half - 1:
            moving_behind = lax.ppermute(moving_behind, "z", behind)
            from_ahead.append(moving_behind)
        if step == 1:
            moving_ahead, moving_behind, pair = lax.optimization_barrier(
                (moving_ahead, moving_behind, pair)
            )
    from_core = lax.ppermute(pair, "c", ring_pairs(core_count, 1))
    pieces = jnp.concatenate([pair, from_core], axis=1)
    gate_piece, up_piece, down_piece = pieces[0], pieces[1], pieces[2]
    gathered = [own_chunk] + from_behind + from_ahead
    rows_all = jnp.concatenate(gathered, axis=0)
    gate_part = lax.dot_general(
        rows_all, gate_piece, (((1,), (1,)), ((), ())), preferred_element_type=jnp.float32
    )
    up_part = lax.dot_general(
        rows_all, up_piece, (((1,), (1,)), ((), ())), preferred_element_type=jnp.float32
    )
    inner_units = (jax.nn.silu(gate_part) * up_part).astype(jnp.bfloat16)
    partial_out = jnp.dot(inner_units, down_piece, preferred_element_type=jnp.float32)
    all_tokens = rows_dev * lax.axis_size("expert") * replicas
    gram_scale = experts / (2.0 * micro_count * all_tokens)
    block_rows = col_width // replicas
    pool_core = jnp.arange(core_count, dtype=jnp.int32)[:, None, None]
    pool_lo = jnp.arange(lo_count, dtype=jnp.int32)[None, :, None]
    gram_cols = (
        (hi_index * core_count + pool_core) * col_width
        + (z_index * lo_count + pool_lo) * block_rows
        + jnp.arange(block_rows, dtype=jnp.int32)[None, None, :]
    ).reshape(-1)
    picker = (jnp.arange(model_width, dtype=jnp.int32)[:, None] == gram_cols[None, :]).astype(
        jnp.bfloat16
    )
    left = jnp.dot(rows_all, picker, preferred_element_type=jnp.float32).astype(jnp.bfloat16)
    product = (
        lax.dot_general(left, rows_all, (((0,), (0,)), ((), ())), preferred_element_type=jnp.float32)
        * gram_scale
    )
    chunks = partial_out.reshape(z_count, -1, hi_count, col_width * core_count)

    def ring_reduce(pieces_z, held):
        forward = pieces_z[half]
        for k in range(1, half + 1):
            if k > 1:
                forward = forward_in.astype(jnp.float32) + pieces_z[2 * half + 1 - k]
            if k == 2 and held is not None:
                forward, held = lax.optimization_barrier((forward, held))
            forward_in = lax.ppermute(forward.astype(jnp.bfloat16), "z", ahead)
        backward = pieces_z[half - 1]
        for k in range(1, half):
            if k > 1:
                backward = backward_in.astype(jnp.float32) + pieces_z[half - k]
            backward_in = lax.ppermute(backward.astype(jnp.bfloat16), "z", behind)
        total = pieces_z[0] + forward_in.astype(jnp.float32) + backward_in.astype(jnp.float32)
        return total, held

    other_cols = lax.dynamic_index_in_dim(chunks, 1 - hi_index, 2, keepdims=False)
    other_sum, product = ring_reduce(other_cols, product)
    swapped = lax.ppermute(other_sum.astype(jnp.bfloat16), "xh", ring_pairs(hi_count, 1))
    mine_cols = lax.dynamic_index_in_dim(chunks, hi_index, 2, keepdims=False)
    mine_cols, other_sum = lax.optimization_barrier((mine_cols, other_sum))
    mine_sum, _ = ring_reduce(mine_cols, None)
    own_half = (mine_sum + swapped.astype(jnp.float32)).astype(jnp.bfloat16)
    by_cols = jnp.moveaxis(own_half.reshape(-1, core_count, col_width), 1, 0)
    by_parts = lax.all_to_all(by_cols, "c", split_axis=0, concat_axis=0, tiled=True)
    by_parts = by_parts.reshape(core_count, micro_count, experts, part, col_width)
    expert_out = jnp.moveaxis(by_parts, 0, 2).reshape(micro_count, experts, capacity, col_width)
    returned = lax.all_to_all(expert_out, "expert", split_axis=1, concat_axis=1, tiled=True)
    flat_back = returned.reshape(micro_count, experts * capacity, col_width)
    first_rows = jnp.take_along_axis(flat_back, target[:, :, 0][:, :, None], axis=1).astype(
        jnp.float32
    )
    second_rows = jnp.take_along_axis(flat_back, target[:, :, 1][:, :, None], axis=1).astype(
        jnp.float32
    )
    own_cols = lax.dynamic_slice_in_dim(tokens, section_index * col_width, col_width, 2).astype(
        jnp.float32
    )
    layer_out = (
        own_cols + first_gate[..., None] * first_rows + second_gate[..., None] * second_rows
    ).astype(jnp.bfloat16)
    gram_block = lax.psum_scatter(
        product.astype(jnp.bfloat16), ("c", "xl"), scatter_dimension=0, tiled=True
    )
    return (layer_out, gram_block[None])


def solution(mesh):
    section, expert, dp = mesh.devices.shape
    fine = Mesh(
        mesh.devices.reshape(2, section // 2, expert, dp // 2, 2), ("xh", "c", "expert", "z", "xl")
    )
    tokens_spec = P(None, ("expert", "z", "xl"), None)
    weight_spec = P("expert", ("xh", "c", "z", "xl"), None)
    return jax.shard_map(
        on_device,
        mesh=fine,
        in_specs=(tokens_spec, tokens_spec, P(), weight_spec, weight_spec, weight_spec),
        out_specs=(P(None, ("expert", "z", "xl"), ("xh", "c")), weight_spec),
        check_vma=False,
    )
```

```python
import jax
import jax.numpy as jnp
from jax import lax
from jax.sharding import Mesh
from jax.sharding import PartitionSpec as P


def route_targets(route_ids, experts, capacity):
    onehot = (route_ids[:, :, None] == jnp.arange(experts, dtype=jnp.int32)[None, None, :]).astype(
        jnp.int32
    )
    flattened = onehot.reshape(-1, experts)
    before = jnp.cumsum(flattened, axis=0) - flattened
    slot_rank = jnp.sum(before * flattened, axis=1).reshape(route_ids.shape)
    return route_ids * capacity + slot_rank


def ring_pairs(count, step):
    return [(i, (i + step) % count) for i in range(count)]


def on_device(tokens, routes, router, gate_weight, up_weight, down_weight):
    micro_count = tokens.shape[0]
    rows_dev = tokens.shape[1]
    model_width = tokens.shape[2]
    experts = router.shape[1]
    capacity = 9 * rows_dev // (4 * experts)
    hi_count = lax.axis_size("xh")
    core_count = lax.axis_size("c")
    z_count = lax.axis_size("z")
    lo_count = lax.axis_size("xl")
    section_count = hi_count * core_count
    replicas = z_count * lo_count
    hi_index = lax.axis_index("xh")
    core_index = lax.axis_index("c")
    z_index = lax.axis_index("z")
    lo_index = lax.axis_index("xl")
    section_index = hi_index * core_count + core_index
    col_width = model_width // section_count
    part = capacity // core_count
    logits = jnp.einsum("mtd,de->mte", tokens, router, preferred_element_type=jnp.float32)
    chosen = jnp.take_along_axis(logits, routes, axis=-1)
    logit_gap = chosen[..., 0] - chosen[..., 1]
    first_gate = jax.nn.sigmoid(logit_gap)
    second_gate = jax.nn.sigmoid(-logit_gap)
    target = jax.vmap(lambda one_block: route_targets(one_block, experts, capacity))(routes)
    slot_ids = (
        jnp.arange(experts, dtype=jnp.int32)[:, None] * capacity
        + core_index * part
        + jnp.arange(part, dtype=jnp.int32)[None, :]
    ).reshape(-1)
    placing = jnp.sum(
        (slot_ids[None, :, None, None] == target[:, None, :, :]).astype(jnp.float32), axis=3
    ).astype(jnp.bfloat16)
    outgoing = jnp.einsum(
        "mst,mtd->msd", placing, tokens, preferred_element_type=jnp.float32
    ).astype(jnp.bfloat16)
    outgoing = outgoing.reshape(micro_count, experts, part, model_width)
    arrived = lax.all_to_all(outgoing, "expert", split_axis=1, concat_axis=1, tiled=True)
    own_chunk = arrived.reshape(-1, model_width)
    stacked = jnp.stack([gate_weight[0], up_weight[0], down_weight[0]])
    from_lo = lax.ppermute(stacked, "xl", ring_pairs(lo_count, 1))
    pair = jnp.concatenate([stacked, from_lo], axis=1)
    half = z_count // 2
    ahead = ring_pairs(z_count, 1)
    behind = ring_pairs(z_count, -1)
    from_behind, from_ahead = [], []
    moving_ahead = own_chunk
    moving_behind = own_chunk
    for step in range(half):
        moving_ahead = lax.ppermute(moving_ahead, "z", ahead)
        from_behind.append(moving_ahead)
        if step < half - 1:
            moving_behind = lax.ppermute(moving_behind, "z", behind)
            from_ahead.append(moving_behind)
        if step == 1:
            moving_ahead, moving_behind, pair = lax.optimization_barrier(
                (moving_ahead, moving_behind, pair)
            )
    from_core = lax.ppermute(pair, "c", ring_pairs(core_count, 1))
    pieces = jnp.concatenate([pair, from_core], axis=1)
    gate_piece, up_piece, down_piece = pieces[0], pieces[1], pieces[2]
    gathered = [own_chunk] + from_behind + from_ahead
    rows_all = jnp.concatenate(gathered, axis=0)
    gate_part = lax.dot_general(
        rows_all, gate_piece, (((1,), (1,)), ((), ())), preferred_element_type=jnp.float32
    )
    up_part = lax.dot_general(
        rows_all, up_piece, (((1,), (1,)), ((), ())), preferred_element_type=jnp.float32
    )
    inner_units = (jax.nn.silu(gate_part) * up_part).astype(jnp.bfloat16)
    partial_out = jnp.dot(inner_units, down_piece, preferred_element_type=jnp.float32)
    all_tokens = rows_dev * lax.axis_size("expert") * replicas
    gram_scale = experts / (2.0 * micro_count * all_tokens)
    block_rows = col_width // replicas
    pool_core = jnp.arange(core_count, dtype=jnp.int32)[:, None, None]
    pool_lo = jnp.arange(lo_count, dtype=jnp.int32)[None, :, None]
    gram_cols = (
        (hi_index * core_count + pool_core) * col_width
        + (z_index * lo_count + pool_lo) * block_rows
        + jnp.arange(block_rows, dtype=jnp.int32)[None, None, :]
    ).reshape(-1)
    picker = (jnp.arange(model_width, dtype=jnp.int32)[:, None] == gram_cols[None, :]).astype(
        jnp.bfloat16
    )

    def gram_of(rows):
        left = jnp.dot(rows, picker, preferred_element_type=jnp.float32).astype(jnp.bfloat16)
        return (
            lax.dot_general(left, rows, (((0,), (0,)), ((), ())), preferred_element_type=jnp.float32)
            * gram_scale
        )

    chunks = partial_out.reshape(z_count, -1, hi_count, col_width * core_count)

    def ring_reduce(pieces_z, with_gram):
        held = None
        forward = pieces_z[half]
        for k in range(1, half + 1):
            if k > 1:
                forward = forward_in.astype(jnp.float32) + pieces_z[2 * half + 1 - k]
            if with_gram and k == 2:
                gram_rows, _ = lax.optimization_barrier((rows_all, forward_in))
                held = gram_of(gram_rows)
            if with_gram and k == 3:
                forward, held = lax.optimization_barrier((forward, held))
            forward_in = lax.ppermute(forward.astype(jnp.bfloat16), "z", ahead)
        backward = pieces_z[half - 1]
        for k in range(1, half):
            if k > 1:
                backward = backward_in.astype(jnp.float32) + pieces_z[half - k]
            backward_in = lax.ppermute(backward.astype(jnp.bfloat16), "z", behind)
        total = pieces_z[0] + forward_in.astype(jnp.float32) + backward_in.astype(jnp.float32)
        return total, held

    other_cols = lax.dynamic_index_in_dim(chunks, 1 - hi_index, 2, keepdims=False)
    other_sum, product = ring_reduce(other_cols, True)
    swapped = lax.ppermute(other_sum.astype(jnp.bfloat16), "xh", ring_pairs(hi_count, 1))
    mine_cols = lax.dynamic_index_in_dim(chunks, hi_index, 2, keepdims=False)
    mine_cols, other_sum = lax.optimization_barrier((mine_cols, other_sum))
    mine_sum, _ = ring_reduce(mine_cols, False)
    own_half = (mine_sum + swapped.astype(jnp.float32)).astype(jnp.bfloat16)
    by_cols = jnp.moveaxis(own_half.reshape(-1, core_count, col_width), 1, 0)
    by_parts = lax.all_to_all(by_cols, "c", split_axis=0, concat_axis=0, tiled=True)
    by_parts = by_parts.reshape(core_count, micro_count, experts, part, col_width)
    expert_out = jnp.moveaxis(by_parts, 0, 2).reshape(micro_count, experts, capacity, col_width)
    returned = lax.all_to_all(expert_out, "expert", split_axis=1, concat_axis=1, tiled=True)
    flat_back = returned.reshape(micro_count, experts * capacity, col_width)
    first_rows = jnp.take_along_axis(flat_back, target[:, :, 0][:, :, None], axis=1).astype(
        jnp.float32
    )
    second_rows = jnp.take_along_axis(flat_back, target[:, :, 1][:, :, None], axis=1).astype(
        jnp.float32
    )
    own_cols = lax.dynamic_slice_in_dim(tokens, section_index * col_width, col_width, 2).astype(
        jnp.float32
    )
    layer_out = (
        own_cols + first_gate[..., None] * first_rows + second_gate[..., None] * second_rows
    ).astype(jnp.bfloat16)
    gram_block = lax.psum_scatter(
        product.astype(jnp.bfloat16), ("c", "xl"), scatter_dimension=0, tiled=True
    )
    return (layer_out, gram_block[None])


def solution(mesh):
    section, expert, dp = mesh.devices.shape
    fine = Mesh(
        mesh.devices.reshape(2, section // 2, expert, dp // 2, 2), ("xh", "c", "expert", "z", "xl")
    )
    tokens_spec = P(None, ("expert", "z", "xl"), None)
    weight_spec = P("expert", ("xh", "c", "z", "xl"), None)
    return jax.shard_map(
        on_device,
        mesh=fine,
        in_specs=(tokens_spec, tokens_spec, P(), weight_spec, weight_spec, weight_spec),
        out_specs=(P(None, ("expert", "z", "xl"), ("xh", "c")), weight_spec),
        check_vma=False,
    )
```

```python
import jax
import jax.numpy as jnp
from jax import lax
from jax.sharding import Mesh
from jax.sharding import PartitionSpec as P


def route_targets(route_ids, experts, capacity):
    onehot = (route_ids[:, :, None] == jnp.arange(experts, dtype=jnp.int32)[None, None, :]).astype(
        jnp.int32
    )
    flattened = onehot.reshape(-1, experts)
    before = jnp.cumsum(flattened, axis=0) - flattened
    slot_rank = jnp.sum(before * flattened, axis=1).reshape(route_ids.shape)
    return route_ids * capacity + slot_rank


def ring_pairs(count, step):
    return [(i, (i + step) % count) for i in range(count)]


def on_device(tokens, routes, router, gate_weight, up_weight, down_weight):
    micro_count = tokens.shape[0]
    rows_dev = tokens.shape[1]
    model_width = tokens.shape[2]
    experts = router.shape[1]
    capacity = 9 * rows_dev // (4 * experts)
    hi_count = lax.axis_size("xh")
    core_count = lax.axis_size("c")
    z_count = lax.axis_size("z")
    lo_count = lax.axis_size("xl")
    section_count = hi_count * core_count
    replicas = z_count * lo_count
    hi_index = lax.axis_index("xh")
    core_index = lax.axis_index("c")
    z_index = lax.axis_index("z")
    lo_index = lax.axis_index("xl")
    section_index = hi_index * core_count + core_index
    col_width = model_width // section_count
    part = capacity // core_count
    logits = jnp.einsum("mtd,de->mte", tokens, router, preferred_element_type=jnp.float32)
    chosen = jnp.take_along_axis(logits, routes, axis=-1)
    logit_gap = chosen[..., 0] - chosen[..., 1]
    first_gate = jax.nn.sigmoid(logit_gap)
    second_gate = jax.nn.sigmoid(-logit_gap)
    target = jax.vmap(lambda one_block: route_targets(one_block, experts, capacity))(routes)
    slot_ids = (
        jnp.arange(experts, dtype=jnp.int32)[:, None] * capacity
        + core_index * part
        + jnp.arange(part, dtype=jnp.int32)[None, :]
    ).reshape(-1)
    placing = jnp.sum(
        (slot_ids[None, :, None, None] == target[:, None, :, :]).astype(jnp.float32), axis=3
    ).astype(jnp.bfloat16)
    outgoing = jnp.einsum(
        "mst,mtd->msd", placing, tokens, preferred_element_type=jnp.float32
    ).astype(jnp.bfloat16)
    outgoing = outgoing.reshape(micro_count, experts, part, model_width)
    arrived = lax.all_to_all(outgoing, "expert", split_axis=1, concat_axis=1, tiled=True)
    own_chunk = arrived.reshape(-1, model_width)
    stacked = jnp.stack([gate_weight[0], up_weight[0], down_weight[0]])
    from_lo = lax.ppermute(stacked, "xl", ring_pairs(lo_count, 1))
    pair = jnp.concatenate([stacked, from_lo], axis=1)
    half = z_count // 2
    ahead = ring_pairs(z_count, 1)
    behind = ring_pairs(z_count, -1)
    split = model_width // 2
    from_behind, from_ahead = [], []
    moving_ahead = own_chunk
    moving_behind = own_chunk
    for step in range(half):
        if step < half - 1:
            moving_ahead = lax.ppermute(moving_ahead, "z", ahead)
            moving_behind = lax.ppermute(moving_behind, "z", behind)
            from_behind.append(moving_ahead)
            from_ahead.append(moving_behind)
        else:
            far_left = lax.ppermute(moving_ahead[:, :split], "z", ahead)
            far_right = lax.ppermute(moving_behind[:, split:], "z", behind)
            from_behind.append(jnp.concatenate([far_left, far_right], axis=1))
        if step == 1:
            moving_ahead, moving_behind, pair = lax.optimization_barrier(
                (moving_ahead, moving_behind, pair)
            )
    from_core = lax.ppermute(pair, "c", ring_pairs(core_count, 1))
    pieces = jnp.concatenate([pair, from_core], axis=1)
    gate_piece, up_piece, down_piece = pieces[0], pieces[1], pieces[2]
    gathered = [own_chunk] + from_behind + from_ahead
    rows_all = jnp.concatenate(gathered, axis=0)
    gate_part = lax.dot_general(
        rows_all, gate_piece, (((1,), (1,)), ((), ())), preferred_element_type=jnp.float32
    )
    up_part = lax.dot_general(
        rows_all, up_piece, (((1,), (1,)), ((), ())), preferred_element_type=jnp.float32
    )
    inner_units = (jax.nn.silu(gate_part) * up_part).astype(jnp.bfloat16)
    partial_out = jnp.dot(inner_units, down_piece, preferred_element_type=jnp.float32)
    all_tokens = rows_dev * lax.axis_size("expert") * replicas
    gram_scale = experts / (2.0 * micro_count * all_tokens)
    block_rows = col_width // replicas
    pool_core = jnp.arange(core_count, dtype=jnp.int32)[:, None, None]
    pool_lo = jnp.arange(lo_count, dtype=jnp.int32)[None, :, None]
    gram_cols = (
        (hi_index * core_count + pool_core) * col_width
        + (z_index * lo_count + pool_lo) * block_rows
        + jnp.arange(block_rows, dtype=jnp.int32)[None, None, :]
    ).reshape(-1)
    picker = (jnp.arange(model_width, dtype=jnp.int32)[:, None] == gram_cols[None, :]).astype(
        jnp.bfloat16
    )

    def gram_of(rows):
        left = jnp.dot(rows, picker, preferred_element_type=jnp.float32).astype(jnp.bfloat16)
        return (
            lax.dot_general(left, rows, (((0,), (0,)), ((), ())), preferred_element_type=jnp.float32)
            * gram_scale
        )

    chunks = partial_out.reshape(z_count, -1, model_width)
    left_part = chunks[:, :, :split]
    right_part = chunks[:, :, split:]
    product = None
    for k in range(1, half + 1):
        if k == 1:
            forward = left_part[half]
            backward = right_part[half]
        else:
            ahead_idx = 2 * half + 1 - k
            behind_idx = half + 1 - k
            if k == 2:
                fwd_left = forward_in.astype(jnp.float32) + left_part[ahead_idx]
                bwd_right = backward_in.astype(jnp.float32) + right_part[behind_idx]
                fwd_right = right_part[ahead_idx]
                bwd_left = left_part[behind_idx]
            else:
                fwd_left = forward_in[:, :split].astype(jnp.float32) + left_part[ahead_idx]
                bwd_right = backward_in[:, split:].astype(jnp.float32) + right_part[behind_idx]
                fwd_right = forward_in[:, split:].astype(jnp.float32) + right_part[ahead_idx]
                bwd_left = backward_in[:, :split].astype(jnp.float32) + left_part[behind_idx]
            forward = jnp.concatenate([fwd_left, fwd_right], axis=1)
            backward = jnp.concatenate([bwd_left, bwd_right], axis=1)
        if k == 2:
            gram_rows, _ = lax.optimization_barrier((rows_all, forward_in))
            product = gram_of(gram_rows)
        if k == 3:
            forward, product = lax.optimization_barrier((forward, product))
        forward_in = lax.ppermute(forward.astype(jnp.bfloat16), "z", ahead)
        backward_in = lax.ppermute(backward.astype(jnp.bfloat16), "z", behind)
    summed = chunks[0] + forward_in.astype(jnp.float32) + backward_in.astype(jnp.float32)
    halves = summed.reshape(-1, hi_count, col_width * core_count)
    other = lax.dynamic_index_in_dim(halves, 1 - hi_index, 1, keepdims=False)
    mine = lax.dynamic_index_in_dim(halves, hi_index, 1, keepdims=False)
    swapped = lax.ppermute(other.astype(jnp.bfloat16), "xh", ring_pairs(hi_count, 1))
    own_half = (mine + swapped.astype(jnp.float32)).astype(jnp.bfloat16)
    by_cols = jnp.moveaxis(own_half.reshape(-1, core_count, col_width), 1, 0)
    by_parts = lax.all_to_all(by_cols, "c", split_axis=0, concat_axis=0, tiled=True)
    by_parts = by_parts.reshape(core_count, micro_count, experts, part, col_width)
    expert_out = jnp.moveaxis(by_parts, 0, 2).reshape(micro_count, experts, capacity, col_width)
    returned = lax.all_to_all(expert_out, "expert", split_axis=1, concat_axis=1, tiled=True)
    flat_back = returned.reshape(micro_count, experts * capacity, col_width)
    first_rows = jnp.take_along_axis(flat_back, target[:, :, 0][:, :, None], axis=1).astype(
        jnp.float32
    )
    second_rows = jnp.take_along_axis(flat_back, target[:, :, 1][:, :, None], axis=1).astype(
        jnp.float32
    )
    own_cols = lax.dynamic_slice_in_dim(tokens, section_index * col_width, col_width, 2).astype(
        jnp.float32
    )
    layer_out = (
        own_cols + first_gate[..., None] * first_rows + second_gate[..., None] * second_rows
    ).astype(jnp.bfloat16)
    gram_block = lax.psum_scatter(
        product.astype(jnp.bfloat16), ("c", "xl"), scatter_dimension=0, tiled=True
    )
    return (layer_out, gram_block[None])


def solution(mesh):
    section, expert, dp = mesh.devices.shape
    fine = Mesh(
        mesh.devices.reshape(2, section // 2, expert, dp // 2, 2), ("xh", "c", "expert", "z", "xl")
    )
    tokens_spec = P(None, ("expert", "z", "xl"), None)
    weight_spec = P("expert", ("xh", "c", "z", "xl"), None)
    return jax.shard_map(
        on_device,
        mesh=fine,
        in_specs=(tokens_spec, tokens_spec, P(), weight_spec, weight_spec, weight_spec),
        out_specs=(P(None, ("expert", "z", "xl"), ("xh", "c")), weight_spec),
        check_vma=False,
    )
```

```python
import jax
import jax.numpy as jnp
from jax import lax
from jax.sharding import Mesh
from jax.sharding import PartitionSpec as P


def route_targets(route_ids, experts, capacity):
    onehot = (route_ids[:, :, None] == jnp.arange(experts, dtype=jnp.int32)[None, None, :]).astype(
        jnp.int32
    )
    flattened = onehot.reshape(-1, experts)
    before = jnp.cumsum(flattened, axis=0) - flattened
    slot_rank = jnp.sum(before * flattened, axis=1).reshape(route_ids.shape)
    return route_ids * capacity + slot_rank


def ring_pairs(count, step):
    return [(i, (i + step) % count) for i in range(count)]


def on_device(tokens, routes, router, gate_weight, up_weight, down_weight):
    micro_count = tokens.shape[0]
    rows_dev = tokens.shape[1]
    model_width = tokens.shape[2]
    experts = router.shape[1]
    capacity = 9 * rows_dev // (4 * experts)
    hi_count = lax.axis_size("xh")
    core_count = lax.axis_size("c")
    z_count = lax.axis_size("z")
    lo_count = lax.axis_size("xl")
    section_count = hi_count * core_count
    replicas = z_count * lo_count
    hi_index = lax.axis_index("xh")
    core_index = lax.axis_index("c")
    z_index = lax.axis_index("z")
    lo_index = lax.axis_index("xl")
    section_index = hi_index * core_count + core_index
    col_width = model_width // section_count
    part = capacity // core_count
    logits = jnp.einsum("mtd,de->mte", tokens, router, preferred_element_type=jnp.float32)
    chosen = jnp.take_along_axis(logits, routes, axis=-1)
    logit_gap = chosen[..., 0] - chosen[..., 1]
    first_gate = jax.nn.sigmoid(logit_gap)
    second_gate = jax.nn.sigmoid(-logit_gap)
    target = jax.vmap(lambda one_block: route_targets(one_block, experts, capacity))(routes)
    slot_ids = (
        jnp.arange(experts, dtype=jnp.int32)[:, None] * capacity
        + core_index * part
        + jnp.arange(part, dtype=jnp.int32)[None, :]
    ).reshape(-1)
    placing = jnp.sum(
        (slot_ids[None, :, None, None] == target[:, None, :, :]).astype(jnp.float32), axis=3
    ).astype(jnp.bfloat16)
    outgoing = jnp.einsum(
        "mst,mtd->msd", placing, tokens, preferred_element_type=jnp.float32
    ).astype(jnp.bfloat16)
    outgoing = outgoing.reshape(micro_count, experts, part, model_width)
    arrived = lax.all_to_all(outgoing, "expert", split_axis=1, concat_axis=1, tiled=True)
    own_chunk = arrived.reshape(-1, model_width)
    stacked = jnp.stack([gate_weight[0], up_weight[0], down_weight[0]])
    from_lo = lax.ppermute(stacked, "xl", ring_pairs(lo_count, 1))
    pair = jnp.concatenate([stacked, from_lo], axis=1)
    half = z_count // 2
    ahead = ring_pairs(z_count, 1)
    behind = ring_pairs(z_count, -1)
    split = model_width // 2
    from_behind, from_ahead = [], []
    moving_ahead = own_chunk
    moving_behind = own_chunk
    for step in range(half):
        if step < half - 1:
            moving_ahead = lax.ppermute(moving_ahead, "z", ahead)
            moving_behind = lax.ppermute(moving_behind, "z", behind)
            from_behind.append(moving_ahead)
            from_ahead.append(moving_behind)
        else:
            far_left = lax.ppermute(moving_ahead[:, :split], "z", ahead)
            far_right = lax.ppermute(moving_behind[:, split:], "z", behind)
            from_behind.append(jnp.concatenate([far_left, far_right], axis=1))
        if step == 1:
            moving_ahead, moving_behind, pair = lax.optimization_barrier(
                (moving_ahead, moving_behind, pair)
            )
    from_core = lax.ppermute(pair, "c", ring_pairs(core_count, 1))
    pieces = jnp.concatenate([pair, from_core], axis=1)
    gate_piece, up_piece, down_piece = pieces[0], pieces[1], pieces[2]
    gathered = [own_chunk] + from_behind + from_ahead
    rows_all = jnp.concatenate(gathered, axis=0)
    gate_part = lax.dot_general(
        rows_all, gate_piece, (((1,), (1,)), ((), ())), preferred_element_type=jnp.float32
    )
    up_part = lax.dot_general(
        rows_all, up_piece, (((1,), (1,)), ((), ())), preferred_element_type=jnp.float32
    )
    inner_units = (jax.nn.silu(gate_part) * up_part).astype(jnp.bfloat16)
    partial_out = jnp.dot(inner_units, down_piece, preferred_element_type=jnp.float32)
    all_tokens = rows_dev * lax.axis_size("expert") * replicas
    gram_scale = experts / (2.0 * micro_count * all_tokens)
    block_rows = col_width // replicas
    pool_core = jnp.arange(core_count, dtype=jnp.int32)[:, None, None]
    pool_lo = jnp.arange(lo_count, dtype=jnp.int32)[None, :, None]
    gram_cols = (
        (hi_index * core_count + pool_core) * col_width
        + (z_index * lo_count + pool_lo) * block_rows
        + jnp.arange(block_rows, dtype=jnp.int32)[None, None, :]
    ).reshape(-1)
    picker = (jnp.arange(model_width, dtype=jnp.int32)[:, None] == gram_cols[None, :]).astype(
        jnp.bfloat16
    )

    def gram_of(rows):
        left = jnp.dot(rows, picker, preferred_element_type=jnp.float32).astype(jnp.bfloat16)
        return (
            lax.dot_general(left, rows, (((0,), (0,)), ((), ())), preferred_element_type=jnp.float32)
            * gram_scale
        )

    chunks = partial_out.reshape(z_count, -1, hi_count, col_width * core_count)

    def ring_reduce(pieces_z, with_gram):
        held = None
        forward = pieces_z[half]
        for k in range(1, half + 1):
            if k > 1:
                forward = forward_in.astype(jnp.float32) + pieces_z[2 * half + 1 - k]
            if with_gram and k == 2:
                gram_rows, _ = lax.optimization_barrier((rows_all, forward_in))
                held = gram_of(gram_rows)
            if with_gram and k == 3:
                forward, held = lax.optimization_barrier((forward, held))
            forward_in = lax.ppermute(forward.astype(jnp.bfloat16), "z", ahead)
        backward = pieces_z[half - 1]
        for k in range(1, half):
            if k > 1:
                backward = backward_in.astype(jnp.float32) + pieces_z[half - k]
            backward_in = lax.ppermute(backward.astype(jnp.bfloat16), "z", behind)
        total = pieces_z[0] + forward_in.astype(jnp.float32) + backward_in.astype(jnp.float32)
        return total, held

    other_cols = lax.dynamic_index_in_dim(chunks, 1 - hi_index, 2, keepdims=False)
    other_sum, product = ring_reduce(other_cols, True)
    swapped = lax.ppermute(other_sum.astype(jnp.bfloat16), "xh", ring_pairs(hi_count, 1))
    mine_cols = lax.dynamic_index_in_dim(chunks, hi_index, 2, keepdims=False)
    mine_cols, other_sum = lax.optimization_barrier((mine_cols, other_sum))
    mine_sum, _ = ring_reduce(mine_cols, False)
    own_half = (mine_sum + swapped.astype(jnp.float32)).astype(jnp.bfloat16)
    by_cols = jnp.moveaxis(own_half.reshape(-1, core_count, col_width), 1, 0)
    by_parts = lax.all_to_all(by_cols, "c", split_axis=0, concat_axis=0, tiled=True)
    by_parts = by_parts.reshape(core_count, micro_count, experts, part, col_width)
    expert_out = jnp.moveaxis(by_parts, 0, 2).reshape(micro_count, experts, capacity, col_width)
    returned = lax.all_to_all(expert_out, "expert", split_axis=1, concat_axis=1, tiled=True)
    flat_back = returned.reshape(micro_count, experts * capacity, col_width)
    first_rows = jnp.take_along_axis(flat_back, target[:, :, 0][:, :, None], axis=1).astype(
        jnp.float32
    )
    second_rows = jnp.take_along_axis(flat_back, target[:, :, 1][:, :, None], axis=1).astype(
        jnp.float32
    )
    own_cols = lax.dynamic_slice_in_dim(tokens, section_index * col_width, col_width, 2).astype(
        jnp.float32
    )
    layer_out = (
        own_cols + first_gate[..., None] * first_rows + second_gate[..., None] * second_rows
    ).astype(jnp.bfloat16)
    gram_block = lax.psum_scatter(
        product.astype(jnp.bfloat16), ("c", "xl"), scatter_dimension=0, tiled=True
    )
    return (layer_out, gram_block[None])


def solution(mesh):
    section, expert, dp = mesh.devices.shape
    fine = Mesh(
        mesh.devices.reshape(2, section // 2, expert, dp // 2, 2), ("xh", "c", "expert", "z", "xl")
    )
    tokens_spec = P(None, ("expert", "z", "xl"), None)
    weight_spec = P("expert", ("xh", "c", "z", "xl"), None)
    return jax.shard_map(
        on_device,
        mesh=fine,
        in_specs=(tokens_spec, tokens_spec, P(), weight_spec, weight_spec, weight_spec),
        out_specs=(P(None, ("expert", "z", "xl"), ("xh", "c")), weight_spec),
        check_vma=False,
    )
```

```python
import jax
import jax.numpy as jnp
from jax import lax
from jax.sharding import Mesh
from jax.sharding import PartitionSpec as P


def route_targets(route_ids, experts, capacity):
    onehot = (route_ids[:, :, None] == jnp.arange(experts, dtype=jnp.int32)[None, None, :]).astype(
        jnp.int32
    )
    flattened = onehot.reshape(-1, experts)
    before = jnp.cumsum(flattened, axis=0) - flattened
    slot_rank = jnp.sum(before * flattened, axis=1).reshape(route_ids.shape)
    return route_ids * capacity + slot_rank


def ring_pairs(count, step):
    return [(i, (i + step) % count) for i in range(count)]


def on_device(tokens, routes, router, gate_weight, up_weight, down_weight):
    micro_count = tokens.shape[0]
    rows_dev = tokens.shape[1]
    model_width = tokens.shape[2]
    experts = router.shape[1]
    capacity = 9 * rows_dev // (4 * experts)
    hi_count = lax.axis_size("xh")
    core_count = lax.axis_size("c")
    z_count = lax.axis_size("z")
    lo_count = lax.axis_size("xl")
    section_count = hi_count * core_count
    replicas = z_count * lo_count
    hi_index = lax.axis_index("xh")
    core_index = lax.axis_index("c")
    z_index = lax.axis_index("z")
    lo_index = lax.axis_index("xl")
    section_index = hi_index * core_count + core_index
    col_width = model_width // section_count
    part = capacity // core_count
    logits = jnp.einsum("mtd,de->mte", tokens, router, preferred_element_type=jnp.float32)
    chosen = jnp.take_along_axis(logits, routes, axis=-1)
    logit_gap = chosen[..., 0] - chosen[..., 1]
    first_gate = jax.nn.sigmoid(logit_gap)
    second_gate = jax.nn.sigmoid(-logit_gap)
    target = jax.vmap(lambda one_block: route_targets(one_block, experts, capacity))(routes)
    slot_ids = (
        jnp.arange(experts, dtype=jnp.int32)[:, None] * capacity
        + core_index * part
        + jnp.arange(part, dtype=jnp.int32)[None, :]
    ).reshape(-1)
    placing = jnp.sum(
        (slot_ids[None, :, None, None] == target[:, None, :, :]).astype(jnp.float32), axis=3
    ).astype(jnp.bfloat16)
    outgoing = jnp.einsum(
        "mst,mtd->msd", placing, tokens, preferred_element_type=jnp.float32
    ).astype(jnp.bfloat16)
    outgoing = outgoing.reshape(micro_count, experts, part, model_width)
    arrived = lax.all_to_all(outgoing, "expert", split_axis=1, concat_axis=1, tiled=True)
    own_chunk = arrived.reshape(-1, model_width)
    stacked = jnp.stack([gate_weight[0], up_weight[0], down_weight[0]])
    from_lo = lax.ppermute(stacked, "xl", ring_pairs(lo_count, 1))
    pair = jnp.concatenate([stacked, from_lo], axis=1)
    half = z_count // 2
    ahead = ring_pairs(z_count, 1)
    behind = ring_pairs(z_count, -1)
    split = model_width // 2
    from_behind, from_ahead = [], []
    moving_ahead = own_chunk
    moving_behind = own_chunk
    for step in range(half):
        if step < half - 1:
            moving_ahead = lax.ppermute(moving_ahead, "z", ahead)
            moving_behind = lax.ppermute(moving_behind, "z", behind)
            from_behind.append(moving_ahead)
            from_ahead.append(moving_behind)
        else:
            far_left = lax.ppermute(moving_ahead[:, :split], "z", ahead)
            far_right = lax.ppermute(moving_behind[:, split:], "z", behind)
            from_behind.append(jnp.concatenate([far_left, far_right], axis=1))
        if step == 1:
            moving_ahead, moving_behind, pair = lax.optimization_barrier(
                (moving_ahead, moving_behind, pair)
            )
    from_core = lax.ppermute(pair, "c", ring_pairs(core_count, 1))
    pieces = jnp.concatenate([pair, from_core], axis=1)
    gate_piece, up_piece, down_piece = pieces[0], pieces[1], pieces[2]
    gathered = [own_chunk] + from_behind + from_ahead
    rows_all = jnp.concatenate(gathered, axis=0)
    gate_part = lax.dot_general(
        rows_all, gate_piece, (((1,), (1,)), ((), ())), preferred_element_type=jnp.float32
    )
    up_part = lax.dot_general(
        rows_all, up_piece, (((1,), (1,)), ((), ())), preferred_element_type=jnp.float32
    )
    inner_units = (jax.nn.silu(gate_part) * up_part).astype(jnp.bfloat16)
    partial_out = jnp.dot(inner_units, down_piece, preferred_element_type=jnp.float32)
    all_tokens = rows_dev * lax.axis_size("expert") * replicas
    gram_scale = experts / (2.0 * micro_count * all_tokens)
    block_rows = col_width // replicas
    pool_core = jnp.arange(core_count, dtype=jnp.int32)[:, None, None]
    pool_lo = jnp.arange(lo_count, dtype=jnp.int32)[None, :, None]
    gram_cols = (
        (hi_index * core_count + pool_core) * col_width
        + (z_index * lo_count + pool_lo) * block_rows
        + jnp.arange(block_rows, dtype=jnp.int32)[None, None, :]
    ).reshape(-1)
    picker = (jnp.arange(model_width, dtype=jnp.int32)[:, None] == gram_cols[None, :]).astype(
        jnp.bfloat16
    )

    def gram_of(rows):
        left = jnp.dot(rows, picker, preferred_element_type=jnp.float32).astype(jnp.bfloat16)
        return (
            lax.dot_general(left, rows, (((0,), (0,)), ((), ())), preferred_element_type=jnp.float32)
            * gram_scale
        )

    chunks = partial_out.reshape(z_count, -1, model_width)
    forward = chunks[half]
    backward = chunks[half - 1]
    for k in range(1, half + 1):
        if k > 1:
            forward = forward_in.astype(jnp.float32) + chunks[2 * half + 1 - k]
        if 1 < k < half:
            backward = backward_in.astype(jnp.float32) + chunks[half - k]
        if k == 2:
            gram_rows, _ = lax.optimization_barrier((rows_all, forward_in))
            product = gram_of(gram_rows)
        if k == 3:
            forward, product = lax.optimization_barrier((forward, product))
        forward_in = lax.ppermute(forward.astype(jnp.bfloat16), "z", ahead)
        if k < half:
            backward_in = lax.ppermute(backward.astype(jnp.bfloat16), "z", behind)
    summed = chunks[0] + forward_in.astype(jnp.float32) + backward_in.astype(jnp.float32)
    halves = summed.reshape(-1, hi_count, col_width * core_count)
    other = lax.dynamic_index_in_dim(halves, 1 - hi_index, 1, keepdims=False)
    mine = lax.dynamic_index_in_dim(halves, hi_index, 1, keepdims=False)
    swapped = lax.ppermute(other.astype(jnp.bfloat16), "xh", ring_pairs(hi_count, 1))
    own_half = (mine + swapped.astype(jnp.float32)).astype(jnp.bfloat16)
    by_cols = jnp.moveaxis(own_half.reshape(-1, core_count, col_width), 1, 0)
    by_parts = lax.all_to_all(by_cols, "c", split_axis=0, concat_axis=0, tiled=True)
    by_parts = by_parts.reshape(core_count, micro_count, experts, part, col_width)
    expert_out = jnp.moveaxis(by_parts, 0, 2).reshape(micro_count, experts, capacity, col_width)
    returned = lax.all_to_all(expert_out, "expert", split_axis=1, concat_axis=1, tiled=True)
    flat_back = returned.reshape(micro_count, experts * capacity, col_width)
    first_rows = jnp.take_along_axis(flat_back, target[:, :, 0][:, :, None], axis=1).astype(
        jnp.float32
    )
    second_rows = jnp.take_along_axis(flat_back, target[:, :, 1][:, :, None], axis=1).astype(
        jnp.float32
    )
    own_cols = lax.dynamic_slice_in_dim(tokens, section_index * col_width, col_width, 2).astype(
        jnp.float32
    )
    layer_out = (
        own_cols + first_gate[..., None] * first_rows + second_gate[..., None] * second_rows
    ).astype(jnp.bfloat16)
    gram_block = lax.psum_scatter(
        product.astype(jnp.bfloat16), ("c", "xl"), scatter_dimension=0, tiled=True
    )
    return (layer_out, gram_block[None])


def solution(mesh):
    section, expert, dp = mesh.devices.shape
    fine = Mesh(
        mesh.devices.reshape(2, section // 2, expert, dp // 2, 2), ("xh", "c", "expert", "z", "xl")
    )
    tokens_spec = P(None, ("expert", "z", "xl"), None)
    weight_spec = P("expert", ("xh", "c", "z", "xl"), None)
    return jax.shard_map(
        on_device,
        mesh=fine,
        in_specs=(tokens_spec, tokens_spec, P(), weight_spec, weight_spec, weight_spec),
        out_specs=(P(None, ("expert", "z", "xl"), ("xh", "c")), weight_spec),
        check_vma=False,
    )
```

```python
import jax
import jax.numpy as jnp
from jax import lax
from jax.sharding import Mesh
from jax.sharding import PartitionSpec as P


def route_targets(route_ids, experts, capacity):
    onehot = (route_ids[:, :, None] == jnp.arange(experts, dtype=jnp.int32)[None, None, :]).astype(
        jnp.int32
    )
    flattened = onehot.reshape(-1, experts)
    before = jnp.cumsum(flattened, axis=0) - flattened
    slot_rank = jnp.sum(before * flattened, axis=1).reshape(route_ids.shape)
    return route_ids * capacity + slot_rank


def ring_pairs(count, step):
    return [(i, (i + step) % count) for i in range(count)]


def on_device(tokens, routes, router, gate_weight, up_weight, down_weight):
    micro_count = tokens.shape[0]
    rows_dev = tokens.shape[1]
    model_width = tokens.shape[2]
    experts = router.shape[1]
    capacity = 9 * rows_dev // (4 * experts)
    hi_count = lax.axis_size("xh")
    core_count = lax.axis_size("c")
    z_count = lax.axis_size("z")
    lo_count = lax.axis_size("xl")
    section_count = hi_count * core_count
    replicas = z_count * lo_count
    hi_index = lax.axis_index("xh")
    core_index = lax.axis_index("c")
    z_index = lax.axis_index("z")
    lo_index = lax.axis_index("xl")
    section_index = hi_index * core_count + core_index
    col_width = model_width // section_count
    part = capacity // core_count
    logits = jnp.einsum("mtd,de->mte", tokens, router, preferred_element_type=jnp.float32)
    chosen = jnp.take_along_axis(logits, routes, axis=-1)
    logit_gap = chosen[..., 0] - chosen[..., 1]
    first_gate = jax.nn.sigmoid(logit_gap)
    second_gate = jax.nn.sigmoid(-logit_gap)
    target = jax.vmap(lambda one_block: route_targets(one_block, experts, capacity))(routes)
    slot_ids = (
        jnp.arange(experts, dtype=jnp.int32)[:, None] * capacity
        + core_index * part
        + jnp.arange(part, dtype=jnp.int32)[None, :]
    ).reshape(-1)
    placing = jnp.sum(
        (slot_ids[None, :, None, None] == target[:, None, :, :]).astype(jnp.float32), axis=3
    ).astype(jnp.bfloat16)
    outgoing = jnp.einsum(
        "mst,mtd->msd", placing, tokens, preferred_element_type=jnp.float32
    ).astype(jnp.bfloat16)
    outgoing = outgoing.reshape(micro_count, experts, part, model_width)
    expert_count = lax.axis_size("expert")
    expert_index = lax.axis_index("expert")
    by_shift = jnp.roll(outgoing, -expert_index, axis=1)
    arrived = jnp.stack(
        [by_shift[:, 0]]
        + [
            lax.ppermute(by_shift[:, j], "expert", ring_pairs(expert_count, j))
            for j in range(1, expert_count)
        ],
        axis=1,
    )
    own_chunk = arrived.reshape(-1, model_width)
    stacked = jnp.stack([gate_weight[0], up_weight[0], down_weight[0]])
    from_lo = lax.ppermute(stacked, "xl", ring_pairs(lo_count, 1))
    pair = jnp.concatenate([stacked, from_lo], axis=1)
    half = z_count // 2
    ahead = ring_pairs(z_count, 1)
    behind = ring_pairs(z_count, -1)
    split = model_width // 2
    from_behind, from_ahead = [], []
    moving_ahead = own_chunk
    moving_behind = own_chunk
    for step in range(half):
        if step < half - 1:
            moving_ahead = lax.ppermute(moving_ahead, "z", ahead)
            moving_behind = lax.ppermute(moving_behind, "z", behind)
            from_behind.append(moving_ahead)
            from_ahead.append(moving_behind)
        else:
            far_left = lax.ppermute(moving_ahead[:, :split], "z", ahead)
            far_right = lax.ppermute(moving_behind[:, split:], "z", behind)
            from_behind.append(jnp.concatenate([far_left, far_right], axis=1))
        if step == 1:
            moving_ahead, moving_behind, pair = lax.optimization_barrier(
                (moving_ahead, moving_behind, pair)
            )
    from_core = lax.ppermute(pair, "c", ring_pairs(core_count, 1))
    pieces = jnp.concatenate([pair, from_core], axis=1)
    gate_piece, up_piece, down_piece = pieces[0], pieces[1], pieces[2]
    gathered = [own_chunk] + from_behind + from_ahead
    rows_all = jnp.concatenate(gathered, axis=0)
    gate_part = lax.dot_general(
        rows_all, gate_piece, (((1,), (1,)), ((), ())), preferred_element_type=jnp.float32
    )
    up_part = lax.dot_general(
        rows_all, up_piece, (((1,), (1,)), ((), ())), preferred_element_type=jnp.float32
    )
    inner_units = (jax.nn.silu(gate_part) * up_part).astype(jnp.bfloat16)
    partial_out = jnp.dot(inner_units, down_piece, preferred_element_type=jnp.float32)
    all_tokens = rows_dev * lax.axis_size("expert") * replicas
    gram_scale = experts / (2.0 * micro_count * all_tokens)
    block_rows = col_width // replicas
    pool_core = jnp.arange(core_count, dtype=jnp.int32)[:, None, None]
    pool_lo = jnp.arange(lo_count, dtype=jnp.int32)[None, :, None]
    gram_cols = (
        (hi_index * core_count + pool_core) * col_width
        + (z_index * lo_count + pool_lo) * block_rows
        + jnp.arange(block_rows, dtype=jnp.int32)[None, None, :]
    ).reshape(-1)
    picker = (jnp.arange(model_width, dtype=jnp.int32)[:, None] == gram_cols[None, :]).astype(
        jnp.bfloat16
    )

    def gram_of(rows):
        left = jnp.dot(rows, picker, preferred_element_type=jnp.float32).astype(jnp.bfloat16)
        return (
            lax.dot_general(left, rows, (((0,), (0,)), ((), ())), preferred_element_type=jnp.float32)
            * gram_scale
        )

    chunks = partial_out.reshape(z_count, -1, hi_count, col_width * core_count)

    def ring_reduce(pieces_z, with_gram):
        held = None
        forward = pieces_z[half]
        for k in range(1, half + 1):
            if k > 1:
                forward = forward_in.astype(jnp.float32) + pieces_z[2 * half + 1 - k]
            if with_gram and k == 2:
                gram_rows, _ = lax.optimization_barrier((rows_all, forward_in))
                held = gram_of(gram_rows)
            if with_gram and k == 3:
                forward, held = lax.optimization_barrier((forward, held))
            forward_in = lax.ppermute(forward.astype(jnp.bfloat16), "z", ahead)
        backward = pieces_z[half - 1]
        for k in range(1, half):
            if k > 1:
                backward = backward_in.astype(jnp.float32) + pieces_z[half - k]
            backward_in = lax.ppermute(backward.astype(jnp.bfloat16), "z", behind)
        total = pieces_z[0] + forward_in.astype(jnp.float32) + backward_in.astype(jnp.float32)
        return total, held

    other_cols = lax.dynamic_index_in_dim(chunks, 1 - hi_index, 2, keepdims=False)
    other_sum, product = ring_reduce(other_cols, True)
    swapped = lax.ppermute(other_sum.astype(jnp.bfloat16), "xh", ring_pairs(hi_count, 1))
    mine_cols = lax.dynamic_index_in_dim(chunks, hi_index, 2, keepdims=False)
    mine_cols, other_sum = lax.optimization_barrier((mine_cols, other_sum))
    mine_sum, _ = ring_reduce(mine_cols, False)
    own_half = (mine_sum + swapped.astype(jnp.float32)).astype(jnp.bfloat16)
    by_cols = jnp.moveaxis(own_half.reshape(-1, core_count, col_width), 1, 0)
    by_parts = lax.all_to_all(by_cols, "c", split_axis=0, concat_axis=0, tiled=True)
    by_parts = by_parts.reshape(core_count, micro_count, experts, part, col_width)
    expert_out = jnp.moveaxis(by_parts, 0, 2).reshape(micro_count, experts, capacity, col_width)
    back = jnp.stack(
        [expert_out[:, 0]]
        + [
            lax.ppermute(expert_out[:, j], "expert", ring_pairs(expert_count, -j))
            for j in range(1, expert_count)
        ],
        axis=1,
    )
    returned = jnp.roll(back, expert_index, axis=1)
    flat_back = returned.reshape(micro_count, experts * capacity, col_width)
    first_rows = jnp.take_along_axis(flat_back, target[:, :, 0][:, :, None], axis=1).astype(
        jnp.float32
    )
    second_rows = jnp.take_along_axis(flat_back, target[:, :, 1][:, :, None], axis=1).astype(
        jnp.float32
    )
    own_cols = lax.dynamic_slice_in_dim(tokens, section_index * col_width, col_width, 2).astype(
        jnp.float32
    )
    layer_out = (
        own_cols + first_gate[..., None] * first_rows + second_gate[..., None] * second_rows
    ).astype(jnp.bfloat16)
    gram_block = lax.psum_scatter(
        product.astype(jnp.bfloat16), ("c", "xl"), scatter_dimension=0, tiled=True
    )
    return (layer_out, gram_block[None])


def solution(mesh):
    section, expert, dp = mesh.devices.shape
    fine = Mesh(
        mesh.devices.reshape(2, section // 2, expert, dp // 2, 2), ("xh", "c", "expert", "z", "xl")
    )
    tokens_spec = P(None, ("expert", "z", "xl"), None)
    weight_spec = P("expert", ("xh", "c", "z", "xl"), None)
    return jax.shard_map(
        on_device,
        mesh=fine,
        in_specs=(tokens_spec, tokens_spec, P(), weight_spec, weight_spec, weight_spec),
        out_specs=(P(None, ("expert", "z", "xl"), ("xh", "c")), weight_spec),
        check_vma=False,
    )
```

```python
import jax
import jax.numpy as jnp
from jax import lax
from jax.sharding import Mesh
from jax.sharding import PartitionSpec as P


def route_targets(route_ids, experts, capacity):
    onehot = (route_ids[:, :, None] == jnp.arange(experts, dtype=jnp.int32)[None, None, :]).astype(
        jnp.int32
    )
    flattened = onehot.reshape(-1, experts)
    before = jnp.cumsum(flattened, axis=0) - flattened
    slot_rank = jnp.sum(before * flattened, axis=1).reshape(route_ids.shape)
    return route_ids * capacity + slot_rank


def ring_pairs(count, step):
    return [(i, (i + step) % count) for i in range(count)]


def on_device(tokens, routes, router, gate_weight, up_weight, down_weight):
    micro_count = tokens.shape[0]
    rows_dev = tokens.shape[1]
    model_width = tokens.shape[2]
    experts = router.shape[1]
    capacity = 9 * rows_dev // (4 * experts)
    hi_count = lax.axis_size("xh")
    core_count = lax.axis_size("c")
    z_count = lax.axis_size("z")
    lo_count = lax.axis_size("xl")
    section_count = hi_count * core_count
    replicas = z_count * lo_count
    hi_index = lax.axis_index("xh")
    core_index = lax.axis_index("c")
    z_index = lax.axis_index("z")
    lo_index = lax.axis_index("xl")
    section_index = hi_index * core_count + core_index
    col_width = model_width // section_count
    part = capacity // core_count
    logits = jnp.einsum("mtd,de->mte", tokens, router, preferred_element_type=jnp.float32)
    chosen = jnp.take_along_axis(logits, routes, axis=-1)
    logit_gap = chosen[..., 0] - chosen[..., 1]
    first_gate = jax.nn.sigmoid(logit_gap)
    second_gate = jax.nn.sigmoid(-logit_gap)
    target = jax.vmap(lambda one_block: route_targets(one_block, experts, capacity))(routes)
    slot_ids = (
        jnp.arange(experts, dtype=jnp.int32)[:, None] * capacity
        + core_index * part
        + jnp.arange(part, dtype=jnp.int32)[None, :]
    ).reshape(-1)
    placing = jnp.sum(
        (slot_ids[None, :, None, None] == target[:, None, :, :]).astype(jnp.float32), axis=3
    ).astype(jnp.bfloat16)
    outgoing = jnp.einsum(
        "mst,mtd->msd", placing, tokens, preferred_element_type=jnp.float32
    ).astype(jnp.bfloat16)
    outgoing = outgoing.reshape(micro_count, experts, part, model_width)
    expert_count = lax.axis_size("expert")
    expert_index = lax.axis_index("expert")
    by_shift = jnp.roll(outgoing, -expert_index, axis=1)
    received = [by_shift[:, 0]] + [
        lax.ppermute(by_shift[:, j], "expert", ring_pairs(expert_count, j))
        for j in range(1, expert_count)
    ]
    reversed_shifts = jnp.stack([received[(-i) % expert_count] for i in range(expert_count)], axis=1)
    arrived = jnp.roll(reversed_shifts, expert_index, axis=1)
    own_chunk = arrived.reshape(-1, model_width)
    stacked = jnp.stack([gate_weight[0], up_weight[0], down_weight[0]])
    from_lo = lax.ppermute(stacked, "xl", ring_pairs(lo_count, 1))
    pair = jnp.concatenate([stacked, from_lo], axis=1)
    half = z_count // 2
    ahead = ring_pairs(z_count, 1)
    behind = ring_pairs(z_count, -1)
    split = model_width // 2
    from_behind, from_ahead = [], []
    moving_ahead = own_chunk
    moving_behind = own_chunk
    for step in range(half):
        if step < half - 1:
            moving_ahead = lax.ppermute(moving_ahead, "z", ahead)
            moving_behind = lax.ppermute(moving_behind, "z", behind)
            from_behind.append(moving_ahead)
            from_ahead.append(moving_behind)
        else:
            far_left = lax.ppermute(moving_ahead[:, :split], "z", ahead)
            far_right = lax.ppermute(moving_behind[:, split:], "z", behind)
            from_behind.append(jnp.concatenate([far_left, far_right], axis=1))
        if step == 1:
            moving_ahead, moving_behind, pair = lax.optimization_barrier(
                (moving_ahead, moving_behind, pair)
            )
    from_core = lax.ppermute(pair, "c", ring_pairs(core_count, 1))
    pieces = jnp.concatenate([pair, from_core], axis=1)
    gate_piece, up_piece, down_piece = pieces[0], pieces[1], pieces[2]
    gathered = [own_chunk] + from_behind + from_ahead
    rows_all = jnp.concatenate(gathered, axis=0)
    gate_part = lax.dot_general(
        rows_all, gate_piece, (((1,), (1,)), ((), ())), preferred_element_type=jnp.float32
    )
    up_part = lax.dot_general(
        rows_all, up_piece, (((1,), (1,)), ((), ())), preferred_element_type=jnp.float32
    )
    inner_units = (jax.nn.silu(gate_part) * up_part).astype(jnp.bfloat16)
    partial_out = jnp.dot(inner_units, down_piece, preferred_element_type=jnp.float32)
    all_tokens = rows_dev * lax.axis_size("expert") * replicas
    gram_scale = experts / (2.0 * micro_count * all_tokens)
    block_rows = col_width // replicas
    pool_core = jnp.arange(core_count, dtype=jnp.int32)[:, None, None]
    pool_lo = jnp.arange(lo_count, dtype=jnp.int32)[None, :, None]
    gram_cols = (
        (hi_index * core_count + pool_core) * col_width
        + (z_index * lo_count + pool_lo) * block_rows
        + jnp.arange(block_rows, dtype=jnp.int32)[None, None, :]
    ).reshape(-1)
    picker = (jnp.arange(model_width, dtype=jnp.int32)[:, None] == gram_cols[None, :]).astype(
        jnp.bfloat16
    )

    def gram_of(rows):
        left = jnp.dot(rows, picker, preferred_element_type=jnp.float32).astype(jnp.bfloat16)
        return (
            lax.dot_general(left, rows, (((0,), (0,)), ((), ())), preferred_element_type=jnp.float32)
            * gram_scale
        )

    chunks = partial_out.reshape(z_count, -1, hi_count, col_width * core_count)

    def ring_reduce(pieces_z, with_gram):
        held = None
        forward = pieces_z[half]
        for k in range(1, half + 1):
            if k > 1:
                forward = forward_in.astype(jnp.float32) + pieces_z[2 * half + 1 - k]
            if with_gram and k == 2:
                gram_rows, _ = lax.optimization_barrier((rows_all, forward_in))
                held = gram_of(gram_rows)
            if with_gram and k == 3:
                forward, held = lax.optimization_barrier((forward, held))
            forward_in = lax.ppermute(forward.astype(jnp.bfloat16), "z", ahead)
        backward = pieces_z[half - 1]
        for k in range(1, half):
            if k > 1:
                backward = backward_in.astype(jnp.float32) + pieces_z[half - k]
            backward_in = lax.ppermute(backward.astype(jnp.bfloat16), "z", behind)
        total = pieces_z[0] + forward_in.astype(jnp.float32) + backward_in.astype(jnp.float32)
        return total, held

    other_cols = lax.dynamic_index_in_dim(chunks, 1 - hi_index, 2, keepdims=False)
    other_sum, product = ring_reduce(other_cols, True)
    swapped = lax.ppermute(other_sum.astype(jnp.bfloat16), "xh", ring_pairs(hi_count, 1))
    mine_cols = lax.dynamic_index_in_dim(chunks, hi_index, 2, keepdims=False)
    mine_cols, other_sum = lax.optimization_barrier((mine_cols, other_sum))
    mine_sum, _ = ring_reduce(mine_cols, False)
    own_half = (mine_sum + swapped.astype(jnp.float32)).astype(jnp.bfloat16)
    by_cols = jnp.moveaxis(own_half.reshape(-1, core_count, col_width), 1, 0)
    by_parts = lax.all_to_all(by_cols, "c", split_axis=0, concat_axis=0, tiled=True)
    by_parts = by_parts.reshape(core_count, micro_count, experts, part, col_width)
    expert_out = jnp.moveaxis(by_parts, 0, 2).reshape(micro_count, experts, capacity, col_width)
    returned = lax.all_to_all(expert_out, "expert", split_axis=1, concat_axis=1, tiled=True)
    flat_back = returned.reshape(micro_count, experts * capacity, col_width)
    first_rows = jnp.take_along_axis(flat_back, target[:, :, 0][:, :, None], axis=1).astype(
        jnp.float32
    )
    second_rows = jnp.take_along_axis(flat_back, target[:, :, 1][:, :, None], axis=1).astype(
        jnp.float32
    )
    own_cols = lax.dynamic_slice_in_dim(tokens, section_index * col_width, col_width, 2).astype(
        jnp.float32
    )
    layer_out = (
        own_cols + first_gate[..., None] * first_rows + second_gate[..., None] * second_rows
    ).astype(jnp.bfloat16)
    gram_block = lax.psum_scatter(
        product.astype(jnp.bfloat16), ("c", "xl"), scatter_dimension=0, tiled=True
    )
    return (layer_out, gram_block[None])


def solution(mesh):
    section, expert, dp = mesh.devices.shape
    fine = Mesh(
        mesh.devices.reshape(2, section // 2, expert, dp // 2, 2), ("xh", "c", "expert", "z", "xl")
    )
    tokens_spec = P(None, ("expert", "z", "xl"), None)
    weight_spec = P("expert", ("xh", "c", "z", "xl"), None)
    return jax.shard_map(
        on_device,
        mesh=fine,
        in_specs=(tokens_spec, tokens_spec, P(), weight_spec, weight_spec, weight_spec),
        out_specs=(P(None, ("expert", "z", "xl"), ("xh", "c")), weight_spec),
        check_vma=False,
    )
```
